256 devices in a mesh: blk: 32 (over z, y_lo, core), grp: 8 (over x, y_hi).
Axes of the slice: x: 4, y: 4 (y_hi: 2, y_lo: 2; y = y_hi * 2 + y_lo), z: 8, core: 2. Of those that a mesh axis runs over, the one named last changes fastest.
Arguments:
- low_sites: float32 [8, 32768], P(None, ('blk', 'grp')), may hold values from -6 to 6
- low_probes: float32 [8, 32768], P(None, ('blk', 'grp')), may hold values from -0.03314563 to 0.03314563
- high_probes: float32 [8, 16384], P(None, ('blk', 'grp')), may hold values from -0.03314563 to 0.03314563
- nested: int32 [16384], P(('blk', 'grp')), may hold values from 0 to 32767, as said below
- inv_len_low: float32 [8], replicated, may hold values from 0.15 to 0.6
- inv_len_diff: float32 [8], replicated, may hold values from 0.2 to 0.8
Outputs:
- low_out: float32 [8, 32768], P(None, ('blk', 'grp'))
- high_out: float32 [8, 16384], P(None, ('blk', 'grp'))
The draws below stay inside these ranges and needn't reach their ends.
Inputs may be any that keep to these rules, and one draw needn't show every extreme that they name: `nested`: entries are distinct; the high sites in the aligned block of 512 entries number b all lie among the low sites b * 1024 to (b + 1) * 1024 - 1.
All inputs are finite; a program needn't handle non-finite values.
Results may differ from the reference program's by a relative error of at most 0.00021.
Values sent between devices are 32-bit elements; how exact they have to be, the bound alone decides.
No kernel may reach another device: no remote copies, remote signals or barrier semaphores. Data moves between devices by JAX's collectives and lax.ppermute only.
A program may use at most 64 MiB of HBM per device.

```python
import math
import jax
import jax.numpy as jnp
from jax import lax

F = 8
P_SIZE = 8
NL = 32768
NH = 16384
BL = 1024
BH = 512


def draw_nested(key, part):
    block_count = NL // BL

    def one_block(sub):
        first, second = jax.random.split(sub)
        inner = jax.random.permutation(first, BL - 2)[:BH - 2].astype(jnp.int32) + 1
        chosen = jnp.concatenate([inner, jnp.array([0, BL - 1], jnp.int32)])
        return jax.random.permutation(second, chosen)
    keys = jax.random.split(key, block_count)
    lists = jax.vmap(one_block)(keys).astype(jnp.int32)
    offsets = (jnp.arange(block_count, dtype=jnp.int32) * BL)[:, None]
    return (lists + offsets).reshape(-1)


def levels(stream_key, dims, pieces, low, largest):
    factor_of, own = 1.0, jax.random.fold_in(stream_key, 6)
    for axis_at, blocks in pieces:
        steps = jnp.exp(jax.random.uniform(jax.random.fold_in(own, axis_at), (blocks,), jnp.float32, low / len(pieces), largest / len(pieces)))
        factor_of = factor_of * jnp.repeat(steps, dims[axis_at] // blocks).reshape([-1 if axis == axis_at else 1 for axis in range(len(dims))])
    return factor_of


def bell_draw(rng, shape, scale, bound, shards=(), kind=jnp.bfloat16):
    values = jax.random.normal(rng, shape, jnp.float32) * scale
    if len(shards) > 0:
        values = levels(rng, shape, shards, -0.22, 0.18) * values
    return jnp.clip(values, min=-bound, max=bound).astype(kind)


def setup_inputs(seed: int = 0) -> dict:
    key_of = jax.random.split(jax.random.key(seed), 7)
    low_sites = bell_draw(key_of[0], (F, NL), 1.0, 6.0, ((1, 256),), jnp.float32)
    low_probes = bell_draw(key_of[1], (P_SIZE, NL), (NL ** -0.5), 0.03314563, ((1, 256),), jnp.float32)
    high_probes = bell_draw(key_of[2], (P_SIZE, NH), (NL ** -0.5), 0.03314563, ((1, 256),), jnp.float32)
    nested = draw_nested(jax.random.fold_in(key_of[6], 71), 0)
    inv_len_low = jnp.clip(jnp.exp(jax.random.uniform(key_of[4], (F,), jnp.float32, math.log(0.15), math.log(0.6))), 0.15, 0.6)
    inv_len_diff = jnp.clip(jnp.exp(jax.random.uniform(key_of[5], (F,), jnp.float32, math.log(0.2), math.log(0.8))), 0.2, 0.8)
    return dict(low_sites=low_sites, low_probes=low_probes, high_probes=high_probes, nested=nested, inv_len_low=inv_len_low, inv_len_diff=inv_len_diff)


RHO = 0.9
VAR_DIFF = 1.0
SQRT_THREE = 1.7320508075688772

def matern(rows, cols):
    inner = jnp.einsum('fr,fc->rc', rows, cols, precision=lax.Precision.HIGHEST)
    square = lax.optimization_barrier(jnp.sum(rows * rows, 0))[:, None] + lax.optimization_barrier(jnp.sum(cols * cols, 0))[None, :] - 2.0 * inner
    dist = jnp.sqrt(jnp.maximum(square, 0.0))
    return (1.0 + SQRT_THREE * dist) * jnp.exp(-SQRT_THREE * dist)

def partial_product(rows, cols, weights):
    tile = matern(rows, cols)
    return jnp.einsum('pc,rc->pr', weights, tile, precision=lax.Precision.HIGHEST)

def apply_blocked(rows, cols, weights):
    count = cols.shape[1]
    step = math.gcd(count, 2048)
    if step == count:
        return partial_product(rows, cols, weights)
    blocks = count // step
    cols_split = cols.reshape(cols.shape[0], blocks, step).transpose(1, 0, 2)
    weights_split = weights.reshape(weights.shape[0], blocks, step).transpose(1, 0, 2)

    def one_block(total, item):
        return (total + partial_product(rows, item[0], item[1]), None)
    start = jnp.zeros((weights.shape[0], rows.shape[1]), jnp.float32)
    total, _ = lax.scan(one_block, start, (cols_split, weights_split))
    return total

def apply_rows(rows, cols, weights):
    count = rows.shape[1]
    step = math.gcd(count, 1024)
    blocks = count // step
    rows_split = rows.reshape(rows.shape[0], blocks, step).transpose(1, 0, 2)
    parts = lax.map(lambda block: apply_blocked(block, cols, weights), rows_split)
    return parts.transpose(1, 0, 2).reshape(weights.shape[0], count)

def reference(low_sites, low_probes, high_probes, nested, inv_len_low, inv_len_diff):
    index = nested.astype(jnp.int32)
    spread = jnp.zeros_like(low_probes).at[:, index].add(high_probes)
    mixed = low_probes + RHO * spread
    low_cols = low_sites * inv_len_low[:, None]
    low_out = apply_rows(low_cols, low_cols, mixed)
    high_sites = low_sites[:, index]
    high_cols = high_sites * inv_len_diff[:, None]
    discrepancy = VAR_DIFF * apply_rows(high_cols, high_cols, high_probes)
    high_out = RHO * low_out[:, index] + discrepancy
    return (low_out, high_out)
```

```python
import math

import jax
import jax.numpy as jnp
from jax import lax
from jax.sharding import PartitionSpec as P

RHO = 0.9
VAR_DIFF = 1.0
SQRT_THREE = 1.7320508075688772

GRP_BITS = (2, 0, 1)
BLK_BITS = (4, 3, 2, 1, 0)


def matern(rows, cols):
    inner = jnp.einsum("fr,fc->rc", rows, cols, precision=lax.Precision.HIGHEST)
    square = jnp.sum(rows * rows, 0)[:, None] + jnp.sum(cols * cols, 0)[None, :] - 2.0 * inner
    dist = jnp.sqrt(jnp.maximum(square, 0.0))
    return (1.0 + SQRT_THREE * dist) * jnp.exp(-SQRT_THREE * dist)


def partial_product(rows, cols, weights):
    tile = matern(rows, cols)
    return jnp.einsum("pc,rc->pr", weights, tile, precision=lax.Precision.HIGHEST)


def apply_blocked(rows, cols, weights):
    count = cols.shape[1]
    step = math.gcd(count, 2048)
    blocks = count // step
    cols_split = cols.reshape(cols.shape[0], blocks, step).transpose(1, 0, 2)
    weights_split = weights.reshape(weights.shape[0], blocks, step).transpose(1, 0, 2)

    def one_block(total, item):
        return (total + partial_product(rows, item[0], item[1]), None)

    start = jnp.zeros((weights.shape[0], rows.shape[1]), jnp.float32)
    total, _ = lax.scan(one_block, start, (cols_split, weights_split))
    return total


def gather_bits(x, axis, size, bits):
    me = lax.axis_index(axis)
    buf = x[None]
    for bit in bits:
        mask = 1 << bit
        other = lax.ppermute(buf, axis, [(i, i ^ mask) for i in range(size)])
        upper = ((me >> bit) & 1) == 1
        low = jnp.where(upper, other, buf)
        high = jnp.where(upper, buf, other)
        buf = jnp.concatenate([low, high], 0)
    k = len(bits)
    buf = buf.reshape((2,) * k + x.shape)
    order = sorted(range(k), key=lambda i: -bits[k - 1 - i])
    buf = buf.transpose(tuple(order) + tuple(range(k, k + x.ndim)))
    return buf.reshape((size,) + x.shape)


def per_device(low_sites, low_probes, high_probes, nested, inv_len_low, inv_len_diff):
    feats_n, rows_dev = low_sites.shape
    probes_n = low_probes.shape[0]
    highs_dev = high_probes.shape[1]
    grp_size = 1 << len(GRP_BITS)
    blk_size = 1 << len(BLK_BITS)

    packet = jnp.concatenate(
        [low_sites.reshape(-1), low_probes.reshape(-1), high_probes.reshape(-1), nested.astype(jnp.float32)]
    )
    got = gather_bits(packet, "grp", grp_size, GRP_BITS)
    cuts = [feats_n * rows_dev, probes_n * rows_dev, probes_n * highs_dev, highs_dev]
    pieces = []
    start = 0
    for c in cuts:
        pieces.append(got[:, start:start + c])
        start += c

    def unblock(piece, rows):
        return piece.reshape(grp_size, rows, -1).transpose(1, 0, 2).reshape(rows, -1)

    feats_block = unblock(pieces[0], feats_n)
    lowp_block = unblock(pieces[1], probes_n)
    highp_block = unblock(pieces[2], probes_n)
    nest_block = pieces[3].reshape(-1).astype(jnp.int32)

    width = feats_block.shape[1]
    base = lax.axis_index("blk") * width
    place_block = nest_block - base
    slots = lax.broadcasted_iota(jnp.int32, (width,), 0)
    pick = (slots[:, None] == place_block[None, :]).astype(jnp.float32)
    high_feats_block = jnp.dot(
        feats_block, pick, precision=lax.Precision.HIGHEST, preferred_element_type=jnp.float32
    )
    spread = lax.dot_general(
        highp_block, pick, (((1,), (1,)), ((), ())),
        precision=lax.Precision.HIGHEST, preferred_element_type=jnp.float32,
    )
    mixed_block = lowp_block + RHO * spread

    own_high = lax.axis_index("grp") * highs_dev
    high_feats = lax.dynamic_slice_in_dim(high_feats_block, own_high, highs_dev, 1)
    pick_own = lax.dynamic_slice_in_dim(pick, own_high, highs_dev, 1)

    wide = jnp.concatenate([feats_block, mixed_block, high_feats_block, highp_block], 1)
    every = gather_bits(wide, "blk", blk_size, BLK_BITS)
    nb = width
    nh = high_feats_block.shape[1]

    def unstack(part):
        return part.transpose(1, 0, 2).reshape(part.shape[1], -1)

    cols_feat = unstack(every[:, :, :nb])
    cols_weight = unstack(every[:, :, nb:2 * nb])
    cols_high = unstack(every[:, :, 2 * nb:2 * nb + nh])
    cols_hprobe = unstack(every[:, :, 2 * nb + nh:])

    rows_low = low_sites * inv_len_low[:, None]
    rows_diff = high_feats * inv_len_diff[:, None]
    low_cols = cols_feat * inv_len_low[:, None]
    new_low = apply_blocked(rows_low, low_cols, cols_weight)
    new_diff = VAR_DIFF * apply_blocked(rows_diff, cols_high * inv_len_diff[:, None], cols_hprobe)
    low_block = unblock(gather_bits(new_low, "grp", grp_size, GRP_BITS), probes_n)
    high_part = jnp.dot(
        low_block, pick_own, precision=lax.Precision.HIGHEST, preferred_element_type=jnp.float32
    )
    high_out = RHO * high_part + new_diff
    return (new_low, high_out)


def solution(mesh):
    return jax.shard_map(
        per_device,
        mesh=mesh,
        in_specs=(
            P(None, ("blk", "grp")),
            P(None, ("blk", "grp")),
            P(None, ("blk", "grp")),
            P(("blk", "grp")),
            P(),
            P(),
        ),
        out_specs=(P(None, ("blk", "grp")), P(None, ("blk", "grp"))),
        check_vma=False,
    )
```

```python
import math

import jax
import jax.numpy as jnp
from jax import lax
from jax.experimental import pallas as pl
from jax.experimental.pallas import tpu as pltpu
from jax.sharding import PartitionSpec as P

RHO = 0.9
VAR_DIFF = 1.0
SQRT_THREE = 1.7320508075688772

GRP_BITS = (2, 0, 1)
BLK_BITS = (4, 3, 2, 1, 0)


def matern(rows, cols):
    inner = jnp.einsum("fr,fc->rc", rows, cols, precision=lax.Precision.HIGHEST)
    square = jnp.sum(rows * rows, 0)[:, None] + jnp.sum(cols * cols, 0)[None, :] - 2.0 * inner
    dist = jnp.sqrt(jnp.maximum(square, 0.0))
    return (1.0 + SQRT_THREE * dist) * jnp.exp(-SQRT_THREE * dist)


def partial_product(rows, cols, weights):
    tile = matern(rows, cols)
    return jnp.einsum("pc,rc->pr", weights, tile, precision=lax.Precision.HIGHEST)


def apply_blocked(rows, cols, weights):
    count = cols.shape[1]
    step = math.gcd(count, 2048)
    blocks = count // step
    cols_split = cols.reshape(cols.shape[0], blocks, step).transpose(1, 0, 2)
    weights_split = weights.reshape(weights.shape[0], blocks, step).transpose(1, 0, 2)

    def one_block(total, item):
        return (total + partial_product(rows, item[0], item[1]), None)

    start = jnp.zeros((weights.shape[0], rows.shape[1]), jnp.float32)
    total, _ = lax.scan(one_block, start, (cols_split, weights_split))
    return total


COL_TILE = 4096
COL_SUB = 512


def _matvec_kernel(rows_ref, cols_ref, w_ref, out_ref):
    @pl.when(pl.program_id(0) == 0)
    def _init():
        out_ref[...] = jnp.zeros(out_ref.shape, jnp.float32)

    rows = rows_ref[...]
    rn = jnp.sum(rows * rows, axis=1, keepdims=True)

    def body(i, acc):
        start = pl.multiple_of(i * COL_SUB, COL_SUB)
        cols = cols_ref[:, pl.ds(start, COL_SUB)]
        w = w_ref[:, pl.ds(start, COL_SUB)]
        inner = jnp.dot(rows, cols, precision=lax.Precision.HIGHEST, preferred_element_type=jnp.float32)
        cn = jnp.sum(cols * cols, axis=0, keepdims=True)
        square = rn + cn - 2.0 * inner
        dist = jnp.sqrt(jnp.maximum(square, 0.0))
        tile = (1.0 + SQRT_THREE * dist) * jnp.exp(-SQRT_THREE * dist)
        return acc + lax.dot_general(
            w, tile, (((1,), (1,)), ((), ())),
            precision=lax.Precision.HIGHEST, preferred_element_type=jnp.float32,
        )

    steps = cols_ref.shape[1] // COL_SUB
    acc = lax.fori_loop(0, steps, body, jnp.zeros(out_ref.shape, jnp.float32))
    out_ref[...] += acc


def apply_fused(rows, cols, weights, interpret=False):
    feats, count = cols.shape
    nrows = rows.shape[1]
    probes = weights.shape[0]
    tile = min(COL_TILE, count)
    return pl.pallas_call(
        _matvec_kernel,
        grid=(count // tile,),
        in_specs=[
            pl.BlockSpec((nrows, feats), lambda j: (0, 0)),
            pl.BlockSpec((feats, tile), lambda j: (0, j)),
            pl.BlockSpec((probes, tile), lambda j: (0, j)),
        ],
        out_specs=pl.BlockSpec((probes, nrows), lambda j: (0, 0)),
        out_shape=jax.ShapeDtypeStruct((probes, nrows), jnp.float32),
        compiler_params=pltpu.CompilerParams(dimension_semantics=("arbitrary",)),
        interpret=interpret,
    )(rows.T, cols, weights)


def gather_bits(x, axis, size, bits):
    me = lax.axis_index(axis)
    buf = x[None]
    for bit in bits:
        mask = 1 << bit
        other = lax.ppermute(buf, axis, [(i, i ^ mask) for i in range(size)])
        upper = ((me >> bit) & 1) == 1
        low = jnp.where(upper, other, buf)
        high = jnp.where(upper, buf, other)
        buf = jnp.concatenate([low, high], 0)
    k = len(bits)
    buf = buf.reshape((2,) * k + x.shape)
    order = sorted(range(k), key=lambda i: -bits[k - 1 - i])
    buf = buf.transpose(tuple(order) + tuple(range(k, k + x.ndim)))
    return buf.reshape((size,) + x.shape)


def per_device(low_sites, low_probes, high_probes, nested, inv_len_low, inv_len_diff):
    feats_n, rows_dev = low_sites.shape
    probes_n = low_probes.shape[0]
    highs_dev = high_probes.shape[1]
    grp_size = 1 << len(GRP_BITS)
    blk_size = 1 << len(BLK_BITS)

    packet = jnp.concatenate(
        [low_sites.reshape(-1), low_probes.reshape(-1), high_probes.reshape(-1), nested.astype(jnp.float32)]
    )
    got = gather_bits(packet, "grp", grp_size, GRP_BITS)
    cuts = [feats_n * rows_dev, probes_n * rows_dev, probes_n * highs_dev, highs_dev]
    pieces = []
    start = 0
    for c in cuts:
        pieces.append(got[:, start:start + c])
        start += c

    def unblock(piece, rows):
        return piece.reshape(grp_size, rows, -1).transpose(1, 0, 2).reshape(rows, -1)

    feats_block = unblock(pieces[0], feats_n)
    lowp_block = unblock(pieces[1], probes_n)
    highp_block = unblock(pieces[2], probes_n)
    nest_block = pieces[3].reshape(-1).astype(jnp.int32)

    width = feats_block.shape[1]
    base = lax.axis_index("blk") * width
    place_block = nest_block - base
    slots = lax.broadcasted_iota(jnp.int32, (width,), 0)
    pick = (slots[:, None] == place_block[None, :]).astype(jnp.float32)
    high_feats_block = jnp.dot(
        feats_block, pick, precision=lax.Precision.HIGHEST, preferred_element_type=jnp.float32
    )
    spread = lax.dot_general(
        highp_block, pick, (((1,), (1,)), ((), ())),
        precision=lax.Precision.HIGHEST, preferred_element_type=jnp.float32,
    )
    mixed_block = lowp_block + RHO * spread

    own_high = lax.axis_index("grp") * highs_dev
    high_feats = lax.dynamic_slice_in_dim(high_feats_block, own_high, highs_dev, 1)
    pick_own = lax.dynamic_slice_in_dim(pick, own_high, highs_dev, 1)

    wide = jnp.concatenate([feats_block, mixed_block, high_feats_block, highp_block], 1)
    every = gather_bits(wide, "blk", blk_size, BLK_BITS)
    nb = width
    nh = high_feats_block.shape[1]

    def unstack(part):
        return part.transpose(1, 0, 2).reshape(part.shape[1], -1)

    cols_feat = unstack(every[:, :, :nb])
    cols_weight = unstack(every[:, :, nb:2 * nb])
    cols_high = unstack(every[:, :, 2 * nb:2 * nb + nh])
    cols_hprobe = unstack(every[:, :, 2 * nb + nh:])

    rows_low = low_sites * inv_len_low[:, None]
    rows_diff = high_feats * inv_len_diff[:, None]
    low_cols = cols_feat * inv_len_low[:, None]
    new_low = apply_fused(rows_low, low_cols, cols_weight)
    new_diff = VAR_DIFF * apply_fused(rows_diff, cols_high * inv_len_diff[:, None], cols_hprobe)
    low_block = unblock(gather_bits(new_low, "grp", grp_size, GRP_BITS), probes_n)
    high_part = jnp.dot(
        low_block, pick_own, precision=lax.Precision.HIGHEST, preferred_element_type=jnp.float32
    )
    high_out = RHO * high_part + new_diff
    return (new_low, high_out)


def solution(mesh):
    return jax.shard_map(
        per_device,
        mesh=mesh,
        in_specs=(
            P(None, ("blk", "grp")),
            P(None, ("blk", "grp")),
            P(None, ("blk", "grp")),
            P(("blk", "grp")),
            P(),
            P(),
        ),
        out_specs=(P(None, ("blk", "grp")), P(None, ("blk", "grp"))),
        check_vma=False,
    )
```

```python
import functools

import jax
import jax.numpy as jnp
from jax import lax
from jax.experimental import pallas as pl
from jax.experimental.pallas import tpu as pltpu
from jax.sharding import PartitionSpec as P


RHO = 0.9
VAR_DIFF = 1.0
SQRT_THREE = 1.7320508075688772

GRP_BITS = (2, 0, 1)
BLK_BITS = (4, 3, 2, 1, 0)


COL_SUB = 512


def _accumulate(rows, rn, cols, w):
    inner = jnp.dot(rows, cols, precision=lax.Precision.HIGHEST, preferred_element_type=jnp.float32)
    cn = jnp.sum(cols * cols, axis=0, keepdims=True)
    square = rn + cn - 2.0 * inner
    dist = jnp.sqrt(jnp.maximum(square, 0.0))
    tile = (1.0 + SQRT_THREE * dist) * jnp.exp(-SQRT_THREE * dist)
    return lax.dot_general(
        w, tile, (((1,), (1,)), ((), ())),
        precision=lax.Precision.HIGH, preferred_element_type=jnp.float32,
    )


def _piece_kernel(rl_ref, rd_ref, sl_ref, sd_ref, x_ref, ol_ref, od_ref, *, nb, nh):
    @pl.when(pl.program_id(0) == 0)
    def _init():
        ol_ref[...] = jnp.zeros(ol_ref.shape, jnp.float32)
        od_ref[...] = jnp.zeros(od_ref.shape, jnp.float32)

    rows_l = rl_ref[...]
    rows_d = rd_ref[...]
    rn_l = jnp.sum(rows_l * rows_l, axis=1, keepdims=True)
    rn_d = jnp.sum(rows_d * rows_d, axis=1, keepdims=True)
    scale_l = sl_ref[...]
    scale_d = sd_ref[...]

    def one_block(b, carry):
        acc_l, acc_d = carry
        for c in range(0, nb, COL_SUB):
            cols = x_ref[b, :, c:c + COL_SUB] * scale_l
            w = x_ref[b, :, nb + c:nb + c + COL_SUB]
            acc_l = acc_l + _accumulate(rows_l, rn_l, cols, w)
        for c in range(0, nh, COL_SUB):
            cols = x_ref[b, :, 2 * nb + c:2 * nb + c + COL_SUB] * scale_d
            w = x_ref[b, :, 2 * nb + nh + c:2 * nb + nh + c + COL_SUB]
            acc_d = acc_d + _accumulate(rows_d, rn_d, cols, w)
        return acc_l, acc_d

    zero_l = jnp.zeros(ol_ref.shape, jnp.float32)
    zero_d = jnp.zeros(od_ref.shape, jnp.float32)
    acc_l, acc_d = lax.fori_loop(0, x_ref.shape[0], one_block, (zero_l, zero_d))
    ol_ref[...] += acc_l
    od_ref[...] += acc_d


def apply_piece(rows_low, rows_diff, inv_len_low, inv_len_diff, piece, nb, nh, interpret=False):
    n, feats, width = piece.shape
    probes = piece.shape[1]
    per = min(n, 4)
    rl, rd = rows_low.shape[1], rows_diff.shape[1]
    kern = functools.partial(_piece_kernel, nb=nb, nh=nh)
    full = lambda shape: pl.BlockSpec(shape, lambda j: (0,) * len(shape))
    return pl.pallas_call(
        kern,
        grid=(n // per,),
        in_specs=[
            full((rl, feats)),
            full((rd, feats)),
            full((feats, 1)),
            full((feats, 1)),
            pl.BlockSpec((per, feats, width), lambda j: (j, 0, 0)),
        ],
        out_specs=[full((probes, rl)), full((probes, rd))],
        out_shape=[
            jax.ShapeDtypeStruct((probes, rl), jnp.float32),
            jax.ShapeDtypeStruct((probes, rd), jnp.float32),
        ],
        compiler_params=pltpu.CompilerParams(dimension_semantics=("arbitrary",)),
        interpret=interpret,
    )(rows_low.T, rows_diff.T, inv_len_low[:, None], inv_len_diff[:, None], piece)


def gather_bits(x, axis, size, bits):
    me = lax.axis_index(axis)
    buf = x[None]
    for bit in bits:
        mask = 1 << bit
        other = lax.ppermute(buf, axis, [(i, i ^ mask) for i in range(size)])
        upper = ((me >> bit) & 1) == 1
        low = jnp.where(upper, other, buf)
        high = jnp.where(upper, buf, other)
        buf = jnp.concatenate([low, high], 0)
    k = len(bits)
    buf = buf.reshape((2,) * k + x.shape)
    order = sorted(range(k), key=lambda i: -bits[k - 1 - i])
    buf = buf.transpose(tuple(order) + tuple(range(k, k + x.ndim)))
    return buf.reshape((size,) + x.shape)


def per_device(low_sites, low_probes, high_probes, nested, inv_len_low, inv_len_diff):
    feats_n, rows_dev = low_sites.shape
    probes_n = low_probes.shape[0]
    highs_dev = high_probes.shape[1]
    grp_size = 1 << len(GRP_BITS)
    blk_size = 1 << len(BLK_BITS)

    packet = jnp.concatenate(
        [low_sites.reshape(-1), low_probes.reshape(-1), high_probes.reshape(-1), nested.astype(jnp.float32)]
    )
    got = gather_bits(packet, "grp", grp_size, GRP_BITS)
    cuts = [feats_n * rows_dev, probes_n * rows_dev, probes_n * highs_dev, highs_dev]
    pieces = []
    start = 0
    for c in cuts:
        pieces.append(got[:, start:start + c])
        start += c

    def unblock(piece, rows):
        return piece.reshape(grp_size, rows, -1).transpose(1, 0, 2).reshape(rows, -1)

    feats_block = unblock(pieces[0], feats_n)
    lowp_block = unblock(pieces[1], probes_n)
    highp_block = unblock(pieces[2], probes_n)
    nest_block = pieces[3].reshape(-1).astype(jnp.int32)

    width = feats_block.shape[1]
    base = lax.axis_index("blk") * width
    place_block = nest_block - base
    slots = lax.broadcasted_iota(jnp.int32, (width,), 0)
    pick = (slots[:, None] == place_block[None, :]).astype(jnp.float32)
    high_feats_block = jnp.dot(
        feats_block, pick, precision=lax.Precision.HIGHEST, preferred_element_type=jnp.float32
    )
    spread = lax.dot_general(
        highp_block, pick, (((1,), (1,)), ((), ())),
        precision=lax.Precision.HIGHEST, preferred_element_type=jnp.float32,
    )
    mixed_block = lowp_block + RHO * spread

    own_high = lax.axis_index("grp") * highs_dev
    high_feats = lax.dynamic_slice_in_dim(high_feats_block, own_high, highs_dev, 1)
    pick_own = lax.dynamic_slice_in_dim(pick, own_high, highs_dev, 1)

    wide = jnp.concatenate([feats_block, mixed_block, high_feats_block, highp_block], 1)
    nb = width
    nh = high_feats_block.shape[1]
    rows_low = low_sites * inv_len_low[:, None]
    rows_diff = high_feats * inv_len_diff[:, None]

    buf = wide[None]
    new_low, new_diff = apply_piece(rows_low, rows_diff, inv_len_low, inv_len_diff, buf, nb, nh)
    for bit in BLK_BITS:
        mask = 1 << bit
        other = lax.ppermute(buf, "blk", [(i, i ^ mask) for i in range(blk_size)])
        part_low, part_diff = apply_piece(rows_low, rows_diff, inv_len_low, inv_len_diff, other, nb, nh)
        new_low = new_low + part_low
        new_diff = new_diff + part_diff
        if bit != BLK_BITS[-1]:
            buf = jnp.concatenate([buf, other], 0)
    new_diff = VAR_DIFF * new_diff
    low_block = unblock(gather_bits(new_low, "grp", grp_size, GRP_BITS), probes_n)
    high_part = jnp.dot(
        low_block, pick_own, precision=lax.Precision.HIGHEST, preferred_element_type=jnp.float32
    )
    high_out = RHO * high_part + new_diff
    return (new_low, high_out)


def solution(mesh):
    return jax.shard_map(
        per_device,
        mesh=mesh,
        in_specs=(
            P(None, ("blk", "grp")),
            P(None, ("blk", "grp")),
            P(None, ("blk", "grp")),
            P(("blk", "grp")),
            P(),
            P(),
        ),
        out_specs=(P(None, ("blk", "grp")), P(None, ("blk", "grp"))),
        check_vma=False,
    )
```

```python
import functools

import jax
import jax.numpy as jnp
from jax import lax
from jax.experimental import pallas as pl
from jax.experimental.pallas import tpu as pltpu
from jax.sharding import PartitionSpec as P


RHO = 0.9
VAR_DIFF = 1.0
SQRT_THREE = 1.7320508075688772


GRP_BITS = (2, 0, 1)
BLK_BITS = (4, 3, 2, 1, 0)


COL_SUB = 512


def _accumulate(rows, rn, cols, w):
    inner = jnp.dot(rows, cols, precision=lax.Precision.HIGHEST, preferred_element_type=jnp.float32)
    cn = jnp.sum(cols * cols, axis=0, keepdims=True)
    square = rn + cn - 2.0 * inner
    dist = jnp.sqrt(jnp.maximum(square, 0.0))
    tile = (1.0 + SQRT_THREE * dist) * jnp.exp(-SQRT_THREE * dist)
    return lax.dot_general(
        w, tile, (((1,), (1,)), ((), ())),
        precision=lax.Precision.HIGH, preferred_element_type=jnp.float32,
    )


def _piece_kernel(rl_ref, rd_ref, sl_ref, sd_ref, x_ref, ol_ref, od_ref, *, nb, nh):
    @pl.when(pl.program_id(0) == 0)
    def _init():
        ol_ref[...] = jnp.zeros(ol_ref.shape, jnp.float32)
        od_ref[...] = jnp.zeros(od_ref.shape, jnp.float32)

    rows_l = rl_ref[...]
    rows_d = rd_ref[...]
    rn_l = jnp.sum(rows_l * rows_l, axis=1, keepdims=True)
    rn_d = jnp.sum(rows_d * rows_d, axis=1, keepdims=True)
    scale_l = sl_ref[...]
    scale_d = sd_ref[...]

    def one_block(b, carry):
        acc_l, acc_d = carry
        for c in range(0, nb, COL_SUB):
            cols = x_ref[b, :, c:c + COL_SUB] * scale_l
            w = x_ref[b, :, nb + c:nb + c + COL_SUB]
            acc_l = acc_l + _accumulate(rows_l, rn_l, cols, w)
        for c in range(0, nh, COL_SUB):
            cols = x_ref[b, :, 2 * nb + c:2 * nb + c + COL_SUB] * scale_d
            w = x_ref[b, :, 2 * nb + nh + c:2 * nb + nh + c + COL_SUB]
            acc_d = acc_d + _accumulate(rows_d, rn_d, cols, w)
        return acc_l, acc_d

    zero_l = jnp.zeros(ol_ref.shape, jnp.float32)
    zero_d = jnp.zeros(od_ref.shape, jnp.float32)
    acc_l, acc_d = lax.fori_loop(0, x_ref.shape[0], one_block, (zero_l, zero_d))
    ol_ref[...] += acc_l
    od_ref[...] += acc_d


def apply_piece(rows_low, rows_diff, inv_len_low, inv_len_diff, piece, nb, nh, interpret=False):
    n, feats, width = piece.shape
    probes = piece.shape[1]
    per = min(n, 4)
    rl, rd = rows_low.shape[1], rows_diff.shape[1]
    kern = functools.partial(_piece_kernel, nb=nb, nh=nh)
    full = lambda shape: pl.BlockSpec(shape, lambda j: (0,) * len(shape))
    return pl.pallas_call(
        kern,
        grid=(n // per,),
        in_specs=[
            full((rl, feats)),
            full((rd, feats)),
            full((feats, 1)),
            full((feats, 1)),
            pl.BlockSpec((per, feats, width), lambda j: (j, 0, 0)),
        ],
        out_specs=[full((probes, rl)), full((probes, rd))],
        out_shape=[
            jax.ShapeDtypeStruct((probes, rl), jnp.float32),
            jax.ShapeDtypeStruct((probes, rd), jnp.float32),
        ],
        compiler_params=pltpu.CompilerParams(dimension_semantics=("arbitrary",)),
        interpret=interpret,
    )(rows_low.T, rows_diff.T, inv_len_low[:, None], inv_len_diff[:, None], piece)


def gather_direct(x, axis, size):
    me = lax.axis_index(axis)
    recv = [x]
    for s in range(1, size):
        recv.append(lax.ppermute(x, axis, [(i, i ^ s) for i in range(size)]))
    stacked = jnp.stack(recv)
    return jnp.take(stacked, me ^ jnp.arange(size, dtype=jnp.int32), axis=0)


def per_device(low_sites, low_probes, high_probes, nested, inv_len_low, inv_len_diff):
    feats_n, rows_dev = low_sites.shape
    probes_n = low_probes.shape[0]
    highs_dev = high_probes.shape[1]
    grp_size = 1 << len(GRP_BITS)
    blk_size = 1 << len(BLK_BITS)

    packet = jnp.concatenate(
        [low_sites.reshape(-1), low_probes.reshape(-1), high_probes.reshape(-1), nested.astype(jnp.float32)]
    )
    got = gather_direct(packet, "grp", grp_size)
    cuts = [feats_n * rows_dev, probes_n * rows_dev, probes_n * highs_dev, highs_dev]
    pieces = []
    start = 0
    for c in cuts:
        pieces.append(got[:, start:start + c])
        start += c

    def unblock(piece, rows):
        return piece.reshape(grp_size, rows, -1).transpose(1, 0, 2).reshape(rows, -1)

    feats_block = unblock(pieces[0], feats_n)
    lowp_block = unblock(pieces[1], probes_n)
    highp_block = unblock(pieces[2], probes_n)
    nest_block = pieces[3].reshape(-1).astype(jnp.int32)

    width = feats_block.shape[1]
    base = lax.axis_index("blk") * width
    place_block = nest_block - base
    slots = lax.broadcasted_iota(jnp.int32, (width,), 0)
    pick = (slots[:, None] == place_block[None, :]).astype(jnp.float32)
    high_feats_block = jnp.dot(
        feats_block, pick, precision=lax.Precision.HIGHEST, preferred_element_type=jnp.float32
    )
    spread = lax.dot_general(
        highp_block, pick, (((1,), (1,)), ((), ())),
        precision=lax.Precision.HIGHEST, preferred_element_type=jnp.float32,
    )
    mixed_block = lowp_block + RHO * spread

    own_high = lax.axis_index("grp") * highs_dev
    high_feats = lax.dynamic_slice_in_dim(high_feats_block, own_high, highs_dev, 1)
    pick_own = lax.dynamic_slice_in_dim(pick, own_high, highs_dev, 1)

    wide = jnp.concatenate([feats_block, mixed_block, high_feats_block, highp_block], 1)
    nb = width
    nh = high_feats_block.shape[1]
    rows_low = low_sites * inv_len_low[:, None]
    rows_diff = high_feats * inv_len_diff[:, None]

    buf = wide[None]
    new_low, new_diff = apply_piece(rows_low, rows_diff, inv_len_low, inv_len_diff, buf, nb, nh)
    for bit in BLK_BITS:
        mask = 1 << bit
        other = lax.ppermute(buf, "blk", [(i, i ^ mask) for i in range(blk_size)])
        part_low, part_diff = apply_piece(rows_low, rows_diff, inv_len_low, inv_len_diff, other, nb, nh)
        new_low = new_low + part_low
        new_diff = new_diff + part_diff
        if bit != BLK_BITS[-1]:
            buf = jnp.concatenate([buf, other], 0)
    new_diff = VAR_DIFF * new_diff
    low_block = unblock(gather_direct(new_low, "grp", grp_size), probes_n)
    high_part = jnp.dot(
        low_block, pick_own, precision=lax.Precision.HIGHEST, preferred_element_type=jnp.float32
    )
    high_out = RHO * high_part + new_diff
    return (new_low, high_out)


def solution(mesh):
    return jax.shard_map(
        per_device,
        mesh=mesh,
        in_specs=(
            P(None, ("blk", "grp")),
            P(None, ("blk", "grp")),
            P(None, ("blk", "grp")),
            P(("blk", "grp")),
            P(),
            P(),
        ),
        out_specs=(P(None, ("blk", "grp")), P(None, ("blk", "grp"))),
        check_vma=False,
    )
```

```python
import functools

import jax
import jax.numpy as jnp
from jax import lax
from jax.experimental import pallas as pl
from jax.experimental.pallas import tpu as pltpu
from jax.sharding import PartitionSpec as P


RHO = 0.9
VAR_DIFF = 1.0
SQRT_THREE = 1.7320508075688772

GRP_BITS = (2, 0, 1)
BLK_BITS = (4, 3, 2, 1, 0)


COL_SUB = 512


def _accumulate(rows, rn, cols, w):
    inner = lax.dot_general(
        cols, rows, (((0,), (0,)), ((), ())),
        precision=lax.Precision.HIGHEST, preferred_element_type=jnp.float32,
    )
    cn = jnp.sum(cols * cols, axis=0, keepdims=True).T
    square = rn + cn - 2.0 * inner
    dist = jnp.sqrt(jnp.maximum(square, 0.0))
    tile = (1.0 + SQRT_THREE * dist) * jnp.exp(-SQRT_THREE * dist)
    return jnp.dot(w, tile, precision=lax.Precision.HIGH, preferred_element_type=jnp.float32)


def _piece_kernel(rl_ref, rd_ref, sl_ref, sd_ref, x_ref, ol_ref, od_ref, *, nb, nh):
    @pl.when(pl.program_id(0) == 0)
    def _init():
        ol_ref[...] = jnp.zeros(ol_ref.shape, jnp.float32)
        od_ref[...] = jnp.zeros(od_ref.shape, jnp.float32)

    rows_l = rl_ref[...]
    rows_d = rd_ref[...]
    rn_l = jnp.sum(rows_l * rows_l, axis=0, keepdims=True)
    rn_d = jnp.sum(rows_d * rows_d, axis=0, keepdims=True)
    scale_l = sl_ref[...]
    scale_d = sd_ref[...]

    def one_block(b, carry):
        acc_l, acc_d = carry
        for c in range(0, nb, COL_SUB):
            cols = x_ref[b, :, c:c + COL_SUB] * scale_l
            w = x_ref[b, :, nb + c:nb + c + COL_SUB]
            acc_l = acc_l + _accumulate(rows_l, rn_l, cols, w)
        for c in range(0, nh, COL_SUB):
            cols = x_ref[b, :, 2 * nb + c:2 * nb + c + COL_SUB] * scale_d
            w = x_ref[b, :, 2 * nb + nh + c:2 * nb + nh + c + COL_SUB]
            acc_d = acc_d + _accumulate(rows_d, rn_d, cols, w)
        return acc_l, acc_d

    zero_l = jnp.zeros(ol_ref.shape, jnp.float32)
    zero_d = jnp.zeros(od_ref.shape, jnp.float32)
    acc_l, acc_d = lax.fori_loop(0, x_ref.shape[0], one_block, (zero_l, zero_d))
    ol_ref[...] += acc_l
    od_ref[...] += acc_d


def apply_piece(rows_low, rows_diff, inv_len_low, inv_len_diff, piece, nb, nh, interpret=False):
    n, feats, width = piece.shape
    probes = piece.shape[1]
    per = min(n, 4)
    rl, rd = rows_low.shape[1], rows_diff.shape[1]
    kern = functools.partial(_piece_kernel, nb=nb, nh=nh)
    full = lambda shape: pl.BlockSpec(shape, lambda j: (0,) * len(shape))
    return pl.pallas_call(
        kern,
        grid=(n // per,),
        in_specs=[
            full((feats, rl)),
            full((feats, rd)),
            full((feats, 1)),
            full((feats, 1)),
            pl.BlockSpec((per, feats, width), lambda j: (j, 0, 0)),
        ],
        out_specs=[full((probes, rl)), full((probes, rd))],
        out_shape=[
            jax.ShapeDtypeStruct((probes, rl), jnp.float32),
            jax.ShapeDtypeStruct((probes, rd), jnp.float32),
        ],
        compiler_params=pltpu.CompilerParams(dimension_semantics=("arbitrary",)),
        interpret=interpret,
    )(rows_low, rows_diff, inv_len_low[:, None], inv_len_diff[:, None], piece)


def gather_bits(x, axis, size, bits):
    me = lax.axis_index(axis)
    buf = x[None]
    for bit in bits:
        mask = 1 << bit
        other = lax.ppermute(buf, axis, [(i, i ^ mask) for i in range(size)])
        upper = ((me >> bit) & 1) == 1
        low = jnp.where(upper, other, buf)
        high = jnp.where(upper, buf, other)
        buf = jnp.concatenate([low, high], 0)
    k = len(bits)
    buf = buf.reshape((2,) * k + x.shape)
    order = sorted(range(k), key=lambda i: -bits[k - 1 - i])
    buf = buf.transpose(tuple(order) + tuple(range(k, k + x.ndim)))
    return buf.reshape((size,) + x.shape)


def per_device(low_sites, low_probes, high_probes, nested, inv_len_low, inv_len_diff):
    feats_n, rows_dev = low_sites.shape
    probes_n = low_probes.shape[0]
    highs_dev = high_probes.shape[1]
    grp_size = 1 << len(GRP_BITS)
    blk_size = 1 << len(BLK_BITS)

    packet = jnp.concatenate(
        [low_sites.reshape(-1), low_probes.reshape(-1), high_probes.reshape(-1), nested.astype(jnp.float32)]
    )
    got = gather_bits(packet, "grp", grp_size, GRP_BITS)
    cuts = [feats_n * rows_dev, probes_n * rows_dev, probes_n * highs_dev, highs_dev]
    pieces = []
    start = 0
    for c in cuts:
        pieces.append(got[:, start:start + c])
        start += c

    def unblock(piece, rows):
        return piece.reshape(grp_size, rows, -1).transpose(1, 0, 2).reshape(rows, -1)

    feats_block = unblock(pieces[0], feats_n)
    lowp_block = unblock(pieces[1], probes_n)
    highp_block = unblock(pieces[2], probes_n)
    nest_block = pieces[3].reshape(-1).astype(jnp.int32)

    width = feats_block.shape[1]
    base = lax.axis_index("blk") * width
    place_block = nest_block - base
    slots = lax.broadcasted_iota(jnp.int32, (width,), 0)
    pick = (slots[:, None] == place_block[None, :]).astype(jnp.float32)
    high_feats_block = jnp.dot(
        feats_block, pick, precision=lax.Precision.HIGHEST, preferred_element_type=jnp.float32
    )
    spread = lax.dot_general(
        highp_block, pick, (((1,), (1,)), ((), ())),
        precision=lax.Precision.HIGHEST, preferred_element_type=jnp.float32,
    )
    mixed_block = lowp_block + RHO * spread

    own_high = lax.axis_index("grp") * highs_dev
    high_feats = lax.dynamic_slice_in_dim(high_feats_block, own_high, highs_dev, 1)
    pick_own = lax.dynamic_slice_in_dim(pick, own_high, highs_dev, 1)

    wide = jnp.concatenate([feats_block, mixed_block, high_feats_block, highp_block], 1)
    nb = width
    nh = high_feats_block.shape[1]
    rows_low = low_sites * inv_len_low[:, None]
    rows_diff = high_feats * inv_len_diff[:, None]

    buf = wide[None]
    new_low, new_diff = apply_piece(rows_low, rows_diff, inv_len_low, inv_len_diff, buf, nb, nh)
    for bit in BLK_BITS:
        mask = 1 << bit
        other = lax.ppermute(buf, "blk", [(i, i ^ mask) for i in range(blk_size)])
        part_low, part_diff = apply_piece(rows_low, rows_diff, inv_len_low, inv_len_diff, other, nb, nh)
        new_low = new_low + part_low
        new_diff = new_diff + part_diff
        if bit != BLK_BITS[-1]:
            buf = jnp.concatenate([buf, other], 0)
    new_diff = VAR_DIFF * new_diff
    low_block = unblock(gather_bits(new_low, "grp", grp_size, GRP_BITS), probes_n)
    high_part = jnp.dot(
        low_block, pick_own, precision=lax.Precision.HIGHEST, preferred_element_type=jnp.float32
    )
    high_out = RHO * high_part + new_diff
    return (new_low, high_out)


def solution(mesh):
    return jax.shard_map(
        per_device,
        mesh=mesh,
        in_specs=(
            P(None, ("blk", "grp")),
            P(None, ("blk", "grp")),
            P(None, ("blk", "grp")),
            P(("blk", "grp")),
            P(),
            P(),
        ),
        out_specs=(P(None, ("blk", "grp")), P(None, ("blk", "grp"))),
        check_vma=False,
    )
```

```python
import functools

import jax
import jax.numpy as jnp
from jax import lax
from jax.experimental import pallas as pl
from jax.experimental.pallas import tpu as pltpu
from jax.sharding import PartitionSpec as P


RHO = 0.9
VAR_DIFF = 1.0
SQRT_THREE = 1.7320508075688772

GRP_BITS = (2, 0, 1)
BLK_BITS = (4, 3, 2, 1, 0)


COL_SUB = 256


def _accumulate(rows, rn, cols, w):
    inner = jnp.dot(rows, cols, precision=lax.Precision.HIGHEST, preferred_element_type=jnp.float32)
    cn = jnp.sum(cols * cols, axis=0, keepdims=True)
    square = rn + cn - 2.0 * inner
    dist = jnp.sqrt(jnp.maximum(square, 0.0))
    scaled = SQRT_THREE * dist
    tile = (1.0 + scaled) * jnp.exp(-scaled)
    return lax.dot_general(
        w, tile, (((1,), (1,)), ((), ())),
        precision=lax.Precision.HIGH, preferred_element_type=jnp.float32,
    )


def _piece_kernel(rl_ref, rd_ref, sl_ref, sd_ref, x_ref, ol_ref, od_ref, *, nb, nh):
    @pl.when(pl.program_id(0) == 0)
    def _init():
        ol_ref[...] = jnp.zeros(ol_ref.shape, jnp.float32)
        od_ref[...] = jnp.zeros(od_ref.shape, jnp.float32)

    rows_l = rl_ref[...]
    rows_d = rd_ref[...]
    rn_l = jnp.sum(rows_l * rows_l, axis=1, keepdims=True)
    rn_d = jnp.sum(rows_d * rows_d, axis=1, keepdims=True)
    scale_l = sl_ref[...]
    scale_d = sd_ref[...]

    def one_block(b, carry):
        acc_l, acc_d = carry
        for c in range(0, nb, COL_SUB):
            cols = x_ref[b, :, c:c + COL_SUB] * scale_l
            w = x_ref[b, :, nb + c:nb + c + COL_SUB]
            acc_l = acc_l + _accumulate(rows_l, rn_l, cols, w)
        for c in range(0, nh, COL_SUB):
            cols = x_ref[b, :, 2 * nb + c:2 * nb + c + COL_SUB] * scale_d
            w = x_ref[b, :, 2 * nb + nh + c:2 * nb + nh + c + COL_SUB]
            acc_d = acc_d + _accumulate(rows_d, rn_d, cols, w)
        return acc_l, acc_d

    zero_l = jnp.zeros(ol_ref.shape, jnp.float32)
    zero_d = jnp.zeros(od_ref.shape, jnp.float32)
    acc_l, acc_d = lax.fori_loop(0, x_ref.shape[0], one_block, (zero_l, zero_d))
    ol_ref[...] += acc_l
    od_ref[...] += acc_d


def apply_piece(rows_low, rows_diff, inv_len_low, inv_len_diff, piece, nb, nh, interpret=False):
    n, feats, width = piece.shape
    probes = piece.shape[1]
    per = min(n, 4)
    rl, rd = rows_low.shape[1], rows_diff.shape[1]
    kern = functools.partial(_piece_kernel, nb=nb, nh=nh)
    full = lambda shape: pl.BlockSpec(shape, lambda j: (0,) * len(shape))
    return pl.pallas_call(
        kern,
        grid=(n // per,),
        in_specs=[
            full((rl, feats)),
            full((rd, feats)),
            full((feats, 1)),
            full((feats, 1)),
            pl.BlockSpec((per, feats, width), lambda j: (j, 0, 0)),
        ],
        out_specs=[full((probes, rl)), full((probes, rd))],
        out_shape=[
            jax.ShapeDtypeStruct((probes, rl), jnp.float32),
            jax.ShapeDtypeStruct((probes, rd), jnp.float32),
        ],
        compiler_params=pltpu.CompilerParams(dimension_semantics=("arbitrary",)),
        interpret=interpret,
    )(rows_low.T, rows_diff.T, inv_len_low[:, None], inv_len_diff[:, None], piece)


def gather_bits(x, axis, size, bits):
    me = lax.axis_index(axis)
    buf = x[None]
    for bit in bits:
        mask = 1 << bit
        other = lax.ppermute(buf, axis, [(i, i ^ mask) for i in range(size)])
        upper = ((me >> bit) & 1) == 1
        low = jnp.where(upper, other, buf)
        high = jnp.where(upper, buf, other)
        buf = jnp.concatenate([low, high], 0)
    k = len(bits)
    buf = buf.reshape((2,) * k + x.shape)
    order = sorted(range(k), key=lambda i: -bits[k - 1 - i])
    buf = buf.transpose(tuple(order) + tuple(range(k, k + x.ndim)))
    return buf.reshape((size,) + x.shape)


def per_device(low_sites, low_probes, high_probes, nested, inv_len_low, inv_len_diff):
    feats_n, rows_dev = low_sites.shape
    probes_n = low_probes.shape[0]
    highs_dev = high_probes.shape[1]
    grp_size = 1 << len(GRP_BITS)
    blk_size = 1 << len(BLK_BITS)

    packet = jnp.concatenate(
        [low_sites.reshape(-1), low_probes.reshape(-1), high_probes.reshape(-1), nested.astype(jnp.float32)]
    )
    got = gather_bits(packet, "grp", grp_size, GRP_BITS)
    cuts = [feats_n * rows_dev, probes_n * rows_dev, probes_n * highs_dev, highs_dev]
    pieces = []
    start = 0
    for c in cuts:
        pieces.append(got[:, start:start + c])
        start += c

    def unblock(piece, rows):
        return piece.reshape(grp_size, rows, -1).transpose(1, 0, 2).reshape(rows, -1)

    feats_block = unblock(pieces[0], feats_n)
    lowp_block = unblock(pieces[1], probes_n)
    highp_block = unblock(pieces[2], probes_n)
    nest_block = pieces[3].reshape(-1).astype(jnp.int32)

    width = feats_block.shape[1]
    base = lax.axis_index("blk") * width
    place_block = nest_block - base
    slots = lax.broadcasted_iota(jnp.int32, (width,), 0)
    pick = (slots[:, None] == place_block[None, :]).astype(jnp.float32)
    high_feats_block = jnp.dot(
        feats_block, pick, precision=lax.Precision.HIGHEST, preferred_element_type=jnp.float32
    )
    spread = lax.dot_general(
        highp_block, pick, (((1,), (1,)), ((), ())),
        precision=lax.Precision.HIGHEST, preferred_element_type=jnp.float32,
    )
    mixed_block = lowp_block + RHO * spread

    own_high = lax.axis_index("grp") * highs_dev
    high_feats = lax.dynamic_slice_in_dim(high_feats_block, own_high, highs_dev, 1)
    pick_own = lax.dynamic_slice_in_dim(pick, own_high, highs_dev, 1)

    wide = jnp.concatenate([feats_block, mixed_block, high_feats_block, highp_block], 1)
    nb = width
    nh = high_feats_block.shape[1]
    rows_low = low_sites * inv_len_low[:, None]
    rows_diff = high_feats * inv_len_diff[:, None]

    buf = wide[None]
    new_low, new_diff = apply_piece(rows_low, rows_diff, inv_len_low, inv_len_diff, buf, nb, nh)
    for bit in BLK_BITS:
        mask = 1 << bit
        other = lax.ppermute(buf, "blk", [(i, i ^ mask) for i in range(blk_size)])
        part_low, part_diff = apply_piece(rows_low, rows_diff, inv_len_low, inv_len_diff, other, nb, nh)
        new_low = new_low + part_low
        new_diff = new_diff + part_diff
        if bit != BLK_BITS[-1]:
            buf = jnp.concatenate([buf, other], 0)
    new_diff = VAR_DIFF * new_diff
    low_block = unblock(gather_bits(new_low, "grp", grp_size, GRP_BITS), probes_n)
    high_part = jnp.dot(
        low_block, pick_own, precision=lax.Precision.HIGHEST, preferred_element_type=jnp.float32
    )
    high_out = RHO * high_part + new_diff
    return (new_low, high_out)


def solution(mesh):
    return jax.shard_map(
        per_device,
        mesh=mesh,
        in_specs=(
            P(None, ("blk", "grp")),
            P(None, ("blk", "grp")),
            P(None, ("blk", "grp")),
            P(("blk", "grp")),
            P(),
            P(),
        ),
        out_specs=(P(None, ("blk", "grp")), P(None, ("blk", "grp"))),
        check_vma=False,
    )
```

```python
import functools

import jax
import jax.numpy as jnp
from jax import lax
from jax.experimental import pallas as pl
from jax.experimental.pallas import tpu as pltpu
from jax.sharding import PartitionSpec as P


RHO = 0.9
VAR_DIFF = 1.0
SQRT_THREE = 1.7320508075688772

GRP_BITS = (2, 0, 1)
BLK_BITS = (4, 3, 2, 1, 0)


COL_SUB = 1024


def _accumulate(rows, rn, cols, w):
    inner = jnp.dot(rows, cols, precision=lax.Precision.HIGHEST, preferred_element_type=jnp.float32)
    cn = jnp.sum(cols * cols, axis=0, keepdims=True)
    square = rn + cn - 2.0 * inner
    dist = jnp.sqrt(jnp.maximum(square, 0.0))
    tile = (1.0 + SQRT_THREE * dist) * jnp.exp(-SQRT_THREE * dist)
    return lax.dot_general(
        w, tile, (((1,), (1,)), ((), ())),
        precision=lax.Precision.HIGH, preferred_element_type=jnp.float32,
    )


def _piece_kernel(rl_ref, rd_ref, sl_ref, sd_ref, x_ref, ol_ref, od_ref, *, nb, nh):
    @pl.when(pl.program_id(0) == 0)
    def _init():
        ol_ref[...] = jnp.zeros(ol_ref.shape, jnp.float32)
        od_ref[...] = jnp.zeros(od_ref.shape, jnp.float32)

    rows_l = rl_ref[...]
    rows_d = rd_ref[...]
    rn_l = jnp.sum(rows_l * rows_l, axis=1, keepdims=True)
    rn_d = jnp.sum(rows_d * rows_d, axis=1, keepdims=True)
    scale_l = sl_ref[...]
    scale_d = sd_ref[...]

    def one_block(b, carry):
        acc_l, acc_d = carry
        sub_l = min(COL_SUB, nb)
        sub_h = min(COL_SUB, nh)
        for c in range(0, nb, sub_l):
            cols = x_ref[b, :, c:c + sub_l] * scale_l
            w = x_ref[b, :, nb + c:nb + c + sub_l]
            acc_l = acc_l + _accumulate(rows_l, rn_l, cols, w)
        for c in range(0, nh, sub_h):
            cols = x_ref[b, :, 2 * nb + c:2 * nb + c + sub_h] * scale_d
            w = x_ref[b, :, 2 * nb + nh + c:2 * nb + nh + c + sub_h]
            acc_d = acc_d + _accumulate(rows_d, rn_d, cols, w)
        return acc_l, acc_d

    zero_l = jnp.zeros(ol_ref.shape, jnp.float32)
    zero_d = jnp.zeros(od_ref.shape, jnp.float32)
    acc_l, acc_d = lax.fori_loop(0, x_ref.shape[0], one_block, (zero_l, zero_d))
    ol_ref[...] += acc_l
    od_ref[...] += acc_d


def apply_piece(rows_low, rows_diff, inv_len_low, inv_len_diff, piece, nb, nh, interpret=False):
    n, feats, width = piece.shape
    probes = piece.shape[1]
    per = min(n, 4)
    rl, rd = rows_low.shape[1], rows_diff.shape[1]
    kern = functools.partial(_piece_kernel, nb=nb, nh=nh)
    full = lambda shape: pl.BlockSpec(shape, lambda j: (0,) * len(shape))
    return pl.pallas_call(
        kern,
        grid=(n // per,),
        in_specs=[
            full((rl, feats)),
            full((rd, feats)),
            full((feats, 1)),
            full((feats, 1)),
            pl.BlockSpec((per, feats, width), lambda j: (j, 0, 0)),
        ],
        out_specs=[full((probes, rl)), full((probes, rd))],
        out_shape=[
            jax.ShapeDtypeStruct((probes, rl), jnp.float32),
            jax.ShapeDtypeStruct((probes, rd), jnp.float32),
        ],
        compiler_params=pltpu.CompilerParams(dimension_semantics=("arbitrary",)),
        interpret=interpret,
    )(rows_low.T, rows_diff.T, inv_len_low[:, None], inv_len_diff[:, None], piece)


def gather_bits(x, axis, size, bits):
    me = lax.axis_index(axis)
    buf = x[None]
    for bit in bits:
        mask = 1 << bit
        other = lax.ppermute(buf, axis, [(i, i ^ mask) for i in range(size)])
        upper = ((me >> bit) & 1) == 1
        low = jnp.where(upper, other, buf)
        high = jnp.where(upper, buf, other)
        buf = jnp.concatenate([low, high], 0)
    k = len(bits)
    buf = buf.reshape((2,) * k + x.shape)
    order = sorted(range(k), key=lambda i: -bits[k - 1 - i])
    buf = buf.transpose(tuple(order) + tuple(range(k, k + x.ndim)))
    return buf.reshape((size,) + x.shape)


def per_device(low_sites, low_probes, high_probes, nested, inv_len_low, inv_len_diff):
    feats_n, rows_dev = low_sites.shape
    probes_n = low_probes.shape[0]
    highs_dev = high_probes.shape[1]
    grp_size = 1 << len(GRP_BITS)
    blk_size = 1 << len(BLK_BITS)

    packet = jnp.concatenate(
        [low_sites.reshape(-1), low_probes.reshape(-1), high_probes.reshape(-1), nested.astype(jnp.float32)]
    )
    got = gather_bits(packet, "grp", grp_size, GRP_BITS)
    cuts = [feats_n * rows_dev, probes_n * rows_dev, probes_n * highs_dev, highs_dev]
    pieces = []
    start = 0
    for c in cuts:
        pieces.append(got[:, start:start + c])
        start += c

    def unblock(piece, rows):
        return piece.reshape(grp_size, rows, -1).transpose(1, 0, 2).reshape(rows, -1)

    feats_block = unblock(pieces[0], feats_n)
    lowp_block = unblock(pieces[1], probes_n)
    highp_block = unblock(pieces[2], probes_n)
    nest_block = pieces[3].reshape(-1).astype(jnp.int32)

    width = feats_block.shape[1]
    base = lax.axis_index("blk") * width
    place_block = nest_block - base
    slots = lax.broadcasted_iota(jnp.int32, (width,), 0)
    pick = (slots[:, None] == place_block[None, :]).astype(jnp.float32)
    high_feats_block = jnp.dot(
        feats_block, pick, precision=lax.Precision.HIGHEST, preferred_element_type=jnp.float32
    )
    spread = lax.dot_general(
        highp_block, pick, (((1,), (1,)), ((), ())),
        precision=lax.Precision.HIGHEST, preferred_element_type=jnp.float32,
    )
    mixed_block = lowp_block + RHO * spread

    own_high = lax.axis_index("grp") * highs_dev
    high_feats = lax.dynamic_slice_in_dim(high_feats_block, own_high, highs_dev, 1)
    pick_own = lax.dynamic_slice_in_dim(pick, own_high, highs_dev, 1)

    wide = jnp.concatenate([feats_block, mixed_block, high_feats_block, highp_block], 1)
    nb = width
    nh = high_feats_block.shape[1]
    rows_low = low_sites * inv_len_low[:, None]
    rows_diff = high_feats * inv_len_diff[:, None]

    buf = wide[None]
    new_low, new_diff = apply_piece(rows_low, rows_diff, inv_len_low, inv_len_diff, buf, nb, nh)
    for bit in BLK_BITS:
        mask = 1 << bit
        other = lax.ppermute(buf, "blk", [(i, i ^ mask) for i in range(blk_size)])
        part_low, part_diff = apply_piece(rows_low, rows_diff, inv_len_low, inv_len_diff, other, nb, nh)
        new_low = new_low + part_low
        new_diff = new_diff + part_diff
        if bit != BLK_BITS[-1]:
            buf = jnp.concatenate([buf, other], 0)
    new_diff = VAR_DIFF * new_diff
    low_block = unblock(gather_bits(new_low, "grp", grp_size, GRP_BITS), probes_n)
    high_part = jnp.dot(
        low_block, pick_own, precision=lax.Precision.HIGHEST, preferred_element_type=jnp.float32
    )
    high_out = RHO * high_part + new_diff
    return (new_low, high_out)


def solution(mesh):
    return jax.shard_map(
        per_device,
        mesh=mesh,
        in_specs=(
            P(None, ("blk", "grp")),
            P(None, ("blk", "grp")),
            P(None, ("blk", "grp")),
            P(("blk", "grp")),
            P(),
            P(),
        ),
        out_specs=(P(None, ("blk", "grp")), P(None, ("blk", "grp"))),
        check_vma=False,
    )
```

```python
import functools

import jax
import jax.numpy as jnp
from jax import lax
from jax.experimental import pallas as pl
from jax.experimental.pallas import tpu as pltpu
from jax.sharding import PartitionSpec as P


RHO = 0.9
VAR_DIFF = 1.0
SQRT_THREE = 1.7320508075688772

GRP_BITS = (2, 0, 1)
BLK_BITS = (4, 3, 2, 1, 0)


def _accumulate(rows, rn, cols, w):
    inner = jnp.dot(rows, cols, precision=lax.Precision.HIGHEST, preferred_element_type=jnp.float32)
    cn = jnp.sum(cols * cols, axis=0, keepdims=True)
    square = rn + cn - 2.0 * inner
    dist = jnp.sqrt(jnp.maximum(square, 0.0))
    tile = (1.0 + SQRT_THREE * dist) * jnp.exp(-SQRT_THREE * dist)
    return lax.dot_general(
        w, tile, (((1,), (1,)), ((), ())),
        precision=lax.Precision.HIGH, preferred_element_type=jnp.float32,
    )


def _piece_kernel(rl_ref, rd_ref, sl_ref, sd_ref, x_ref, ol_ref, od_ref, *, nb, nh):
    @pl.when(pl.program_id(0) == 0)
    def _init():
        ol_ref[...] = jnp.zeros(ol_ref.shape, jnp.float32)
        od_ref[...] = jnp.zeros(od_ref.shape, jnp.float32)

    rows_l = rl_ref[...]
    rows_d = rd_ref[...]
    rn_l = jnp.sum(rows_l * rows_l, axis=1, keepdims=True)
    rn_d = jnp.sum(rows_d * rows_d, axis=1, keepdims=True)
    scale_l = sl_ref[...]
    scale_d = sd_ref[...]

    group = 2 if x_ref.shape[0] % 2 == 0 else 1

    def take(b, lo, width):
        return jnp.concatenate([x_ref[b * group + i, :, lo:lo + width] for i in range(group)], 1)

    def one_group(b, carry):
        acc_l, acc_d = carry
        cols = take(b, 0, nb) * scale_l
        acc_l = acc_l + _accumulate(rows_l, rn_l, cols, take(b, nb, nb))
        cols = take(b, 2 * nb, nh) * scale_d
        acc_d = acc_d + _accumulate(rows_d, rn_d, cols, take(b, 2 * nb + nh, nh))
        return acc_l, acc_d

    zero_l = jnp.zeros(ol_ref.shape, jnp.float32)
    zero_d = jnp.zeros(od_ref.shape, jnp.float32)
    acc_l, acc_d = lax.fori_loop(0, x_ref.shape[0] // group, one_group, (zero_l, zero_d))
    ol_ref[...] += acc_l
    od_ref[...] += acc_d


def apply_piece(rows_low, rows_diff, inv_len_low, inv_len_diff, piece, nb, nh, interpret=False):
    n, feats, width = piece.shape
    probes = piece.shape[1]
    per = min(n, 4)
    rl, rd = rows_low.shape[1], rows_diff.shape[1]
    kern = functools.partial(_piece_kernel, nb=nb, nh=nh)
    full = lambda shape: pl.BlockSpec(shape, lambda j: (0,) * len(shape))
    return pl.pallas_call(
        kern,
        grid=(n // per,),
        in_specs=[
            full((rl, feats)),
            full((rd, feats)),
            full((feats, 1)),
            full((feats, 1)),
            pl.BlockSpec((per, feats, width), lambda j: (j, 0, 0)),
        ],
        out_specs=[full((probes, rl)), full((probes, rd))],
        out_shape=[
            jax.ShapeDtypeStruct((probes, rl), jnp.float32),
            jax.ShapeDtypeStruct((probes, rd), jnp.float32),
        ],
        compiler_params=pltpu.CompilerParams(dimension_semantics=("arbitrary",)),
        interpret=interpret,
    )(rows_low.T, rows_diff.T, inv_len_low[:, None], inv_len_diff[:, None], piece)


def gather_bits(x, axis, size, bits):
    me = lax.axis_index(axis)
    buf = x[None]
    for bit in bits:
        mask = 1 << bit
        other = lax.ppermute(buf, axis, [(i, i ^ mask) for i in range(size)])
        upper = ((me >> bit) & 1) == 1
        low = jnp.where(upper, other, buf)
        high = jnp.where(upper, buf, other)
        buf = jnp.concatenate([low, high], 0)
    k = len(bits)
    buf = buf.reshape((2,) * k + x.shape)
    order = sorted(range(k), key=lambda i: -bits[k - 1 - i])
    buf = buf.transpose(tuple(order) + tuple(range(k, k + x.ndim)))
    return buf.reshape((size,) + x.shape)


def per_device(low_sites, low_probes, high_probes, nested, inv_len_low, inv_len_diff):
    feats_n, rows_dev = low_sites.shape
    probes_n = low_probes.shape[0]
    highs_dev = high_probes.shape[1]
    grp_size = 1 << len(GRP_BITS)
    blk_size = 1 << len(BLK_BITS)

    packet = jnp.concatenate(
        [low_sites.reshape(-1), low_probes.reshape(-1), high_probes.reshape(-1), nested.astype(jnp.float32)]
    )
    got = gather_bits(packet, "grp", grp_size, GRP_BITS)
    cuts = [feats_n * rows_dev, probes_n * rows_dev, probes_n * highs_dev, highs_dev]
    pieces = []
    start = 0
    for c in cuts:
        pieces.append(got[:, start:start + c])
        start += c

    def unblock(piece, rows):
        return piece.reshape(grp_size, rows, -1).transpose(1, 0, 2).reshape(rows, -1)

    feats_block = unblock(pieces[0], feats_n)
    lowp_block = unblock(pieces[1], probes_n)
    highp_block = unblock(pieces[2], probes_n)
    nest_block = pieces[3].reshape(-1).astype(jnp.int32)

    width = feats_block.shape[1]
    base = lax.axis_index("blk") * width
    place_block = nest_block - base
    slots = lax.broadcasted_iota(jnp.int32, (width,), 0)
    pick = (slots[:, None] == place_block[None, :]).astype(jnp.float32)
    high_feats_block = jnp.dot(
        feats_block, pick, precision=lax.Precision.HIGHEST, preferred_element_type=jnp.float32
    )
    spread = lax.dot_general(
        highp_block, pick, (((1,), (1,)), ((), ())),
        precision=lax.Precision.HIGHEST, preferred_element_type=jnp.float32,
    )
    mixed_block = lowp_block + RHO * spread

    own_high = lax.axis_index("grp") * highs_dev
    high_feats = lax.dynamic_slice_in_dim(high_feats_block, own_high, highs_dev, 1)
    pick_own = lax.dynamic_slice_in_dim(pick, own_high, highs_dev, 1)

    wide = jnp.concatenate([feats_block, mixed_block, high_feats_block, highp_block], 1)
    nb = width
    nh = high_feats_block.shape[1]
    rows_low = low_sites * inv_len_low[:, None]
    rows_diff = high_feats * inv_len_diff[:, None]

    buf = wide[None]
    new_low, new_diff = apply_piece(rows_low, rows_diff, inv_len_low, inv_len_diff, buf, nb, nh)
    for bit in BLK_BITS:
        mask = 1 << bit
        other = lax.ppermute(buf, "blk", [(i, i ^ mask) for i in range(blk_size)])
        part_low, part_diff = apply_piece(rows_low, rows_diff, inv_len_low, inv_len_diff, other, nb, nh)
        new_low = new_low + part_low
        new_diff = new_diff + part_diff
        if bit != BLK_BITS[-1]:
            buf = jnp.concatenate([buf, other], 0)
    new_diff = VAR_DIFF * new_diff
    low_block = unblock(gather_bits(new_low, "grp", grp_size, GRP_BITS), probes_n)
    high_part = jnp.dot(
        low_block, pick_own, precision=lax.Precision.HIGHEST, preferred_element_type=jnp.float32
    )
    high_out = RHO * high_part + new_diff
    return (new_low, high_out)


def solution(mesh):
    return jax.shard_map(
        per_device,
        mesh=mesh,
        in_specs=(
            P(None, ("blk", "grp")),
            P(None, ("blk", "grp")),
            P(None, ("blk", "grp")),
            P(("blk", "grp")),
            P(),
            P(),
        ),
        out_specs=(P(None, ("blk", "grp")), P(None, ("blk", "grp"))),
        check_vma=False,
    )
```

```python
import functools
import math

import jax
import jax.numpy as jnp
from jax import lax
from jax.experimental import pallas as pl
from jax.experimental.pallas import tpu as pltpu
from jax.sharding import PartitionSpec as P


RHO = 0.9
VAR_DIFF = 1.0
SQRT_THREE = 1.7320508075688772

GRP_BITS = (2, 0, 1)
BLK_BITS = (4, 3, 2, 1, 0)


def _accumulate(rows, rn, cols, w):
    inner = jnp.dot(rows, cols, precision=lax.Precision.HIGHEST, preferred_element_type=jnp.float32)
    cn = jnp.sum(cols * cols, axis=0, keepdims=True)
    square = rn + cn - 2.0 * inner
    dist = jnp.sqrt(jnp.maximum(square, 0.0))
    tile = (1.0 + SQRT_THREE * dist) * jnp.exp(-SQRT_THREE * dist)
    return lax.dot_general(
        w, tile, (((1,), (1,)), ((), ())),
        precision=lax.Precision.HIGH, preferred_element_type=jnp.float32,
    )


def _piece_kernel(rl_ref, rd_ref, sl_ref, sd_ref, x_ref, ol_ref, od_ref, *, nb, nh):
    @pl.when(pl.program_id(0) == 0)
    def _init():
        ol_ref[...] = jnp.zeros(ol_ref.shape, jnp.float32)
        od_ref[...] = jnp.zeros(od_ref.shape, jnp.float32)

    rows_l = rl_ref[...]
    rows_d = rd_ref[...]
    rn_l = jnp.sum(rows_l * rows_l, axis=1, keepdims=True)
    rn_d = jnp.sum(rows_d * rows_d, axis=1, keepdims=True)
    scale_l = sl_ref[...]
    scale_d = sd_ref[...]

    group = math.gcd(x_ref.shape[0], 8)

    def take(b, lo, width):
        return jnp.concatenate([x_ref[b * group + i, :, lo:lo + width] for i in range(group)], 1)

    def one_group(b, carry):
        acc_l, acc_d = carry
        cols = take(b, 0, nb) * scale_l
        acc_l = acc_l + _accumulate(rows_l, rn_l, cols, take(b, nb, nb))
        cols = take(b, 2 * nb, nh) * scale_d
        acc_d = acc_d + _accumulate(rows_d, rn_d, cols, take(b, 2 * nb + nh, nh))
        return acc_l, acc_d

    zero_l = jnp.zeros(ol_ref.shape, jnp.float32)
    zero_d = jnp.zeros(od_ref.shape, jnp.float32)
    acc_l, acc_d = lax.fori_loop(0, x_ref.shape[0] // group, one_group, (zero_l, zero_d))
    ol_ref[...] += acc_l
    od_ref[...] += acc_d


def apply_piece(rows_low, rows_diff, inv_len_low, inv_len_diff, piece, nb, nh, interpret=False):
    n, feats, width = piece.shape
    probes = piece.shape[1]
    per = min(n, 8)
    rl, rd = rows_low.shape[1], rows_diff.shape[1]
    kern = functools.partial(_piece_kernel, nb=nb, nh=nh)
    full = lambda shape: pl.BlockSpec(shape, lambda j: (0,) * len(shape))
    return pl.pallas_call(
        kern,
        grid=(n // per,),
        in_specs=[
            full((rl, feats)),
            full((rd, feats)),
            full((feats, 1)),
            full((feats, 1)),
            pl.BlockSpec((per, feats, width), lambda j: (j, 0, 0)),
        ],
        out_specs=[full((probes, rl)), full((probes, rd))],
        out_shape=[
            jax.ShapeDtypeStruct((probes, rl), jnp.float32),
            jax.ShapeDtypeStruct((probes, rd), jnp.float32),
        ],
        compiler_params=pltpu.CompilerParams(dimension_semantics=("arbitrary",)),
        interpret=interpret,
    )(rows_low.T, rows_diff.T, inv_len_low[:, None], inv_len_diff[:, None], piece)


def gather_bits(x, axis, size, bits):
    me = lax.axis_index(axis)
    buf = x[None]
    for bit in bits:
        mask = 1 << bit
        other = lax.ppermute(buf, axis, [(i, i ^ mask) for i in range(size)])
        upper = ((me >> bit) & 1) == 1
        low = jnp.where(upper, other, buf)
        high = jnp.where(upper, buf, other)
        buf = jnp.concatenate([low, high], 0)
    k = len(bits)
    buf = buf.reshape((2,) * k + x.shape)
    order = sorted(range(k), key=lambda i: -bits[k - 1 - i])
    buf = buf.transpose(tuple(order) + tuple(range(k, k + x.ndim)))
    return buf.reshape((size,) + x.shape)


def per_device(low_sites, low_probes, high_probes, nested, inv_len_low, inv_len_diff):
    feats_n, rows_dev = low_sites.shape
    probes_n = low_probes.shape[0]
    highs_dev = high_probes.shape[1]
    grp_size = 1 << len(GRP_BITS)
    blk_size = 1 << len(BLK_BITS)

    packet = jnp.concatenate(
        [low_sites.reshape(-1), low_probes.reshape(-1), high_probes.reshape(-1), nested.astype(jnp.float32)]
    )
    got = gather_bits(packet, "grp", grp_size, GRP_BITS)
    cuts = [feats_n * rows_dev, probes_n * rows_dev, probes_n * highs_dev, highs_dev]
    pieces = []
    start = 0
    for c in cuts:
        pieces.append(got[:, start:start + c])
        start += c

    def unblock(piece, rows):
        return piece.reshape(grp_size, rows, -1).transpose(1, 0, 2).reshape(rows, -1)

    feats_block = unblock(pieces[0], feats_n)
    lowp_block = unblock(pieces[1], probes_n)
    highp_block = unblock(pieces[2], probes_n)
    nest_block = pieces[3].reshape(-1).astype(jnp.int32)

    width = feats_block.shape[1]
    base = lax.axis_index("blk") * width
    place_block = nest_block - base
    slots = lax.broadcasted_iota(jnp.int32, (width,), 0)
    pick = (slots[:, None] == place_block[None, :]).astype(jnp.float32)
    high_feats_block = jnp.dot(
        feats_block, pick, precision=lax.Precision.HIGHEST, preferred_element_type=jnp.float32
    )
    spread = lax.dot_general(
        highp_block, pick, (((1,), (1,)), ((), ())),
        precision=lax.Precision.HIGHEST, preferred_element_type=jnp.float32,
    )
    mixed_block = lowp_block + RHO * spread

    own_high = lax.axis_index("grp") * highs_dev
    high_feats = lax.dynamic_slice_in_dim(high_feats_block, own_high, highs_dev, 1)
    pick_own = lax.dynamic_slice_in_dim(pick, own_high, highs_dev, 1)

    wide = jnp.concatenate([feats_block, mixed_block, high_feats_block, highp_block], 1)
    nb = width
    nh = high_feats_block.shape[1]
    rows_low = low_sites * inv_len_low[:, None]
    rows_diff = high_feats * inv_len_diff[:, None]

    buf = wide[None]
    new_low, new_diff = apply_piece(rows_low, rows_diff, inv_len_low, inv_len_diff, buf, nb, nh)
    for bit in BLK_BITS:
        mask = 1 << bit
        other = lax.ppermute(buf, "blk", [(i, i ^ mask) for i in range(blk_size)])
        part_low, part_diff = apply_piece(rows_low, rows_diff, inv_len_low, inv_len_diff, other, nb, nh)
        new_low = new_low + part_low
        new_diff = new_diff + part_diff
        if bit != BLK_BITS[-1]:
            buf = jnp.concatenate([buf, other], 0)
    new_diff = VAR_DIFF * new_diff
    low_block = unblock(gather_bits(new_low, "grp", grp_size, GRP_BITS), probes_n)
    high_part = jnp.dot(
        low_block, pick_own, precision=lax.Precision.HIGHEST, preferred_element_type=jnp.float32
    )
    high_out = RHO * high_part + new_diff
    return (new_low, high_out)


def solution(mesh):
    return jax.shard_map(
        per_device,
        mesh=mesh,
        in_specs=(
            P(None, ("blk", "grp")),
            P(None, ("blk", "grp")),
            P(None, ("blk", "grp")),
            P(("blk", "grp")),
            P(),
            P(),
        ),
        out_specs=(P(None, ("blk", "grp")), P(None, ("blk", "grp"))),
        check_vma=False,
    )
```

```python
import functools
import math

import jax
import jax.numpy as jnp
from jax import lax
from jax.experimental import pallas as pl
from jax.experimental.pallas import tpu as pltpu
from jax.sharding import PartitionSpec as P


RHO = 0.9
VAR_DIFF = 1.0
SQRT_THREE = 1.7320508075688772

GRP_BITS = (2, 0, 1)
BLK_BITS = (4, 3, 2, 1, 0)


def _accumulate(rows, rn, cols, w):
    inner = jnp.dot(rows, cols, precision=lax.Precision.HIGHEST, preferred_element_type=jnp.float32)
    cn = jnp.sum(cols * cols, axis=0, keepdims=True)
    square = rn + cn - 2.0 * inner
    dist = jnp.sqrt(jnp.maximum(square, 0.0))
    tile = (1.0 + SQRT_THREE * dist) * jnp.exp(-SQRT_THREE * dist)
    return lax.dot_general(
        w, tile, (((1,), (1,)), ((), ())),
        precision=lax.Precision.HIGH, preferred_element_type=jnp.float32,
    )


def _piece_kernel(rl_ref, rd_ref, sl_ref, sd_ref, x_ref, ol_ref, od_ref, *, nb, nh):
    @pl.when(pl.program_id(0) == 0)
    def _init():
        ol_ref[...] = jnp.zeros(ol_ref.shape, jnp.float32)
        od_ref[...] = jnp.zeros(od_ref.shape, jnp.float32)

    rows_l = rl_ref[...]
    rows_d = rd_ref[...]
    rn_l = jnp.sum(rows_l * rows_l, axis=1, keepdims=True)
    rn_d = jnp.sum(rows_d * rows_d, axis=1, keepdims=True)
    scale_l = sl_ref[...]
    scale_d = sd_ref[...]

    group = math.gcd(x_ref.shape[0], 8)

    def take(b, lo, width):
        return jnp.concatenate([x_ref[b * group + i, :, lo:lo + width] for i in range(group)], 1)

    def one_group(b, carry):
        acc_l, acc_d = carry
        cols = take(b, 0, nb) * scale_l
        acc_l = acc_l + _accumulate(rows_l, rn_l, cols, take(b, nb, nb))
        cols = take(b, 2 * nb, nh) * scale_d
        acc_d = acc_d + _accumulate(rows_d, rn_d, cols, take(b, 2 * nb + nh, nh))
        return acc_l, acc_d

    zero_l = jnp.zeros(ol_ref.shape, jnp.float32)
    zero_d = jnp.zeros(od_ref.shape, jnp.float32)
    acc_l, acc_d = lax.fori_loop(0, x_ref.shape[0] // group, one_group, (zero_l, zero_d))
    ol_ref[...] += acc_l
    od_ref[...] += acc_d


def apply_piece(rows_low, rows_diff, inv_len_low, inv_len_diff, piece, nb, nh, interpret=False):
    n, feats, width = piece.shape
    probes = piece.shape[1]
    per = min(n, 8)
    rl, rd = rows_low.shape[1], rows_diff.shape[1]
    kern = functools.partial(_piece_kernel, nb=nb, nh=nh)
    full = lambda shape: pl.BlockSpec(shape, lambda j: (0,) * len(shape))
    return pl.pallas_call(
        kern,
        grid=(n // per,),
        in_specs=[
            full((rl, feats)),
            full((rd, feats)),
            full((feats, 1)),
            full((feats, 1)),
            pl.BlockSpec((per, feats, width), lambda j: (j, 0, 0)),
        ],
        out_specs=[full((probes, rl)), full((probes, rd))],
        out_shape=[
            jax.ShapeDtypeStruct((probes, rl), jnp.float32),
            jax.ShapeDtypeStruct((probes, rd), jnp.float32),
        ],
        compiler_params=pltpu.CompilerParams(dimension_semantics=("arbitrary",)),
        interpret=interpret,
    )(rows_low.T, rows_diff.T, inv_len_low[:, None], inv_len_diff[:, None], piece)


def gather_bits(x, axis, size, bits):
    me = lax.axis_index(axis)
    buf = x[None]
    for bit in bits:
        mask = 1 << bit
        other = lax.ppermute(buf, axis, [(i, i ^ mask) for i in range(size)])
        upper = ((me >> bit) & 1) == 1
        low = jnp.where(upper, other, buf)
        high = jnp.where(upper, buf, other)
        buf = jnp.concatenate([low, high], 0)
    k = len(bits)
    buf = buf.reshape((2,) * k + x.shape)
    order = sorted(range(k), key=lambda i: -bits[k - 1 - i])
    buf = buf.transpose(tuple(order) + tuple(range(k, k + x.ndim)))
    return buf.reshape((size,) + x.shape)


def per_device(low_sites, low_probes, high_probes, nested, inv_len_low, inv_len_diff):
    feats_n, rows_dev = low_sites.shape
    probes_n = low_probes.shape[0]
    highs_dev = high_probes.shape[1]
    grp_size = 1 << len(GRP_BITS)
    blk_size = 1 << len(BLK_BITS)

    packet = jnp.concatenate(
        [low_sites.reshape(-1), low_probes.reshape(-1), high_probes.reshape(-1), nested.astype(jnp.float32)]
    )
    got = gather_bits(packet, "grp", grp_size, GRP_BITS)
    cuts = [feats_n * rows_dev, probes_n * rows_dev, probes_n * highs_dev, highs_dev]
    pieces = []
    start = 0
    for c in cuts:
        pieces.append(got[:, start:start + c])
        start += c

    def unblock(piece, rows):
        return piece.reshape(grp_size, rows, -1).transpose(1, 0, 2).reshape(rows, -1)

    feats_block = unblock(pieces[0], feats_n)
    lowp_block = unblock(pieces[1], probes_n)
    highp_block = unblock(pieces[2], probes_n)
    nest_block = pieces[3].reshape(-1).astype(jnp.int32)

    width = feats_block.shape[1]
    base = lax.axis_index("blk") * width
    place_block = nest_block - base
    slots = lax.broadcasted_iota(jnp.int32, (width,), 0)
    pick = (slots[:, None] == place_block[None, :]).astype(jnp.float32)
    high_feats_block = jnp.dot(
        feats_block, pick, precision=lax.Precision.HIGHEST, preferred_element_type=jnp.float32
    )
    spread = lax.dot_general(
        highp_block, pick, (((1,), (1,)), ((), ())),
        precision=lax.Precision.HIGHEST, preferred_element_type=jnp.float32,
    )
    mixed_block = lowp_block + RHO * spread

    own_high = lax.axis_index("grp") * highs_dev
    high_feats = lax.dynamic_slice_in_dim(high_feats_block, own_high, highs_dev, 1)

    wide = jnp.concatenate([feats_block, mixed_block, high_feats_block, highp_block], 1)
    nb = width
    nh = high_feats_block.shape[1]
    rows_low = jnp.concatenate([low_sites, high_feats], 1) * inv_len_low[:, None]
    rows_diff = high_feats * inv_len_diff[:, None]

    buf = wide[None]
    new_low, new_diff = apply_piece(rows_low, rows_diff, inv_len_low, inv_len_diff, buf, nb, nh)
    for bit in BLK_BITS:
        mask = 1 << bit
        other = lax.ppermute(buf, "blk", [(i, i ^ mask) for i in range(blk_size)])
        part_low, part_diff = apply_piece(rows_low, rows_diff, inv_len_low, inv_len_diff, other, nb, nh)
        new_low = new_low + part_low
        new_diff = new_diff + part_diff
        if bit != BLK_BITS[-1]:
            buf = jnp.concatenate([buf, other], 0)
    new_diff = VAR_DIFF * new_diff
    high_part = new_low[:, rows_dev:]
    high_out = RHO * high_part + new_diff
    return (new_low[:, :rows_dev], high_out)


def solution(mesh):
    return jax.shard_map(
        per_device,
        mesh=mesh,
        in_specs=(
            P(None, ("blk", "grp")),
            P(None, ("blk", "grp")),
            P(None, ("blk", "grp")),
            P(("blk", "grp")),
            P(),
            P(),
        ),
        out_specs=(P(None, ("blk", "grp")), P(None, ("blk", "grp"))),
        check_vma=False,
    )
```

```python
import functools
import math

import jax
import jax.numpy as jnp
from jax import lax
from jax.experimental import pallas as pl
from jax.experimental.pallas import tpu as pltpu
from jax.sharding import PartitionSpec as P


RHO = 0.9
VAR_DIFF = 1.0
SQRT_THREE = 1.7320508075688772

GRP_BITS = (2, 0, 1)
BLK_BITS = (4, 3, 2, 1, 0)


def _accumulate(rows, rn, cols, w):
    inner = jnp.dot(rows, cols, precision=lax.Precision.HIGHEST, preferred_element_type=jnp.float32)
    cn = jnp.sum(cols * cols, axis=0, keepdims=True)
    square = rn + cn - 2.0 * inner
    dist = jnp.sqrt(jnp.maximum(square, 0.0))
    tile = (1.0 + SQRT_THREE * dist) * jnp.exp(-SQRT_THREE * dist)
    return lax.dot_general(
        w, tile, (((1,), (1,)), ((), ())),
        precision=lax.Precision.HIGH, preferred_element_type=jnp.float32,
    )


def _piece_kernel(rl_ref, rd_ref, x_ref, ol_ref, od_ref, *, nb, nh):
    @pl.when(pl.program_id(0) == 0)
    def _init():
        ol_ref[...] = jnp.zeros(ol_ref.shape, jnp.float32)
        od_ref[...] = jnp.zeros(od_ref.shape, jnp.float32)

    rows_l = rl_ref[...]
    rows_d = rd_ref[...]
    rn_l = jnp.sum(rows_l * rows_l, axis=1, keepdims=True)
    rn_d = jnp.sum(rows_d * rows_d, axis=1, keepdims=True)

    group = math.gcd(x_ref.shape[0], 8)

    def take(b, lo, width):
        return jnp.concatenate([x_ref[b * group + i, :, lo:lo + width] for i in range(group)], 1)

    def one_group(b, carry):
        acc_l, acc_d = carry
        cols = take(b, 0, nb)
        acc_l = acc_l + _accumulate(rows_l, rn_l, cols, take(b, nb, nb))
        cols = take(b, 2 * nb, nh)
        acc_d = acc_d + _accumulate(rows_d, rn_d, cols, take(b, 2 * nb + nh, nh))
        return acc_l, acc_d

    zero_l = jnp.zeros(ol_ref.shape, jnp.float32)
    zero_d = jnp.zeros(od_ref.shape, jnp.float32)
    acc_l, acc_d = lax.fori_loop(0, x_ref.shape[0] // group, one_group, (zero_l, zero_d))
    ol_ref[...] += acc_l
    od_ref[...] += acc_d


def apply_piece(rows_low, rows_diff, piece, nb, nh, interpret=False):
    n, feats, width = piece.shape
    probes = piece.shape[1]
    per = min(n, 8)
    rl, rd = rows_low.shape[1], rows_diff.shape[1]
    kern = functools.partial(_piece_kernel, nb=nb, nh=nh)
    full = lambda shape: pl.BlockSpec(shape, lambda j: (0,) * len(shape))
    return pl.pallas_call(
        kern,
        grid=(n // per,),
        in_specs=[
            full((rl, feats)),
            full((rd, feats)),
            pl.BlockSpec((per, feats, width), lambda j: (j, 0, 0)),
        ],
        out_specs=[full((probes, rl)), full((probes, rd))],
        out_shape=[
            jax.ShapeDtypeStruct((probes, rl), jnp.float32),
            jax.ShapeDtypeStruct((probes, rd), jnp.float32),
        ],
        compiler_params=pltpu.CompilerParams(dimension_semantics=("arbitrary",)),
        interpret=interpret,
    )(rows_low.T, rows_diff.T, piece)


def gather_bits(x, axis, size, bits):
    me = lax.axis_index(axis)
    buf = x[None]
    for bit in bits:
        mask = 1 << bit
        other = lax.ppermute(buf, axis, [(i, i ^ mask) for i in range(size)])
        upper = ((me >> bit) & 1) == 1
        low = jnp.where(upper, other, buf)
        high = jnp.where(upper, buf, other)
        buf = jnp.concatenate([low, high], 0)
    k = len(bits)
    buf = buf.reshape((2,) * k + x.shape)
    order = sorted(range(k), key=lambda i: -bits[k - 1 - i])
    buf = buf.transpose(tuple(order) + tuple(range(k, k + x.ndim)))
    return buf.reshape((size,) + x.shape)


def per_device(low_sites, low_probes, high_probes, nested, inv_len_low, inv_len_diff):
    feats_n, rows_dev = low_sites.shape
    probes_n = low_probes.shape[0]
    highs_dev = high_probes.shape[1]
    grp_size = 1 << len(GRP_BITS)
    blk_size = 1 << len(BLK_BITS)

    packet = jnp.concatenate(
        [low_sites.reshape(-1), low_probes.reshape(-1), high_probes.reshape(-1), nested.astype(jnp.float32)]
    )
    got = gather_bits(packet, "grp", grp_size, GRP_BITS)
    cuts = [feats_n * rows_dev, probes_n * rows_dev, probes_n * highs_dev, highs_dev]
    pieces = []
    start = 0
    for c in cuts:
        pieces.append(got[:, start:start + c])
        start += c

    def unblock(piece, rows):
        return piece.reshape(grp_size, rows, -1).transpose(1, 0, 2).reshape(rows, -1)

    feats_block = unblock(pieces[0], feats_n)
    lowp_block = unblock(pieces[1], probes_n)
    highp_block = unblock(pieces[2], probes_n)
    nest_block = pieces[3].reshape(-1).astype(jnp.int32)

    width = feats_block.shape[1]
    base = lax.axis_index("blk") * width
    place_block = nest_block - base
    slots = lax.broadcasted_iota(jnp.int32, (width,), 0)
    pick = (slots[:, None] == place_block[None, :]).astype(jnp.float32)
    high_feats_block = jnp.dot(
        feats_block, pick, precision=lax.Precision.HIGHEST, preferred_element_type=jnp.float32
    )
    spread = lax.dot_general(
        highp_block, pick, (((1,), (1,)), ((), ())),
        precision=lax.Precision.HIGHEST, preferred_element_type=jnp.float32,
    )
    mixed_block = lowp_block + RHO * spread

    own_high = lax.axis_index("grp") * highs_dev
    high_feats = lax.dynamic_slice_in_dim(high_feats_block, own_high, highs_dev, 1)

    wide = jnp.concatenate(
        [feats_block * inv_len_low[:, None], mixed_block, high_feats_block * inv_len_diff[:, None], highp_block], 1
    )
    nb = width
    nh = high_feats_block.shape[1]
    rows_low = jnp.concatenate([low_sites, high_feats], 1) * inv_len_low[:, None]
    rows_diff = high_feats * inv_len_diff[:, None]

    buf = wide[None]
    new_low, new_diff = apply_piece(rows_low, rows_diff, buf, nb, nh)
    for bit in BLK_BITS:
        mask = 1 << bit
        other = lax.ppermute(buf, "blk", [(i, i ^ mask) for i in range(blk_size)])
        part_low, part_diff = apply_piece(rows_low, rows_diff, other, nb, nh)
        new_low = new_low + part_low
        new_diff = new_diff + part_diff
        if bit != BLK_BITS[-1]:
            buf = jnp.concatenate([buf, other], 0)
    new_diff = VAR_DIFF * new_diff
    high_part = new_low[:, rows_dev:]
    high_out = RHO * high_part + new_diff
    return (new_low[:, :rows_dev], high_out)


def solution(mesh):
    return jax.shard_map(
        per_device,
        mesh=mesh,
        in_specs=(
            P(None, ("blk", "grp")),
            P(None, ("blk", "grp")),
            P(None, ("blk", "grp")),
            P(("blk", "grp")),
            P(),
            P(),
        ),
        out_specs=(P(None, ("blk", "grp")), P(None, ("blk", "grp"))),
        check_vma=False,
    )
```

```python
import functools
import math

import jax
import jax.numpy as jnp
from jax import lax
from jax.experimental import pallas as pl
from jax.experimental.pallas import tpu as pltpu
from jax.sharding import PartitionSpec as P


RHO = 0.9
VAR_DIFF = 1.0
SQRT_THREE = 1.7320508075688772

GRP_BITS = (2, 0, 1)
BLK_BITS = (4, 3, 2, 1, 0)


def _accumulate(rows_m2, rn, cols, w):
    inner_m2 = jnp.dot(rows_m2, cols, precision=lax.Precision.HIGHEST, preferred_element_type=jnp.float32)
    cn = jnp.sum(cols * cols, axis=0, keepdims=True)
    square = (rn + cn) + inner_m2
    dist = jnp.sqrt(jnp.maximum(square, 0.0))
    scaled = SQRT_THREE * dist
    tile = (1.0 + scaled) * jnp.exp(-scaled)
    return lax.dot_general(
        w, tile, (((1,), (1,)), ((), ())),
        precision=lax.Precision.HIGH, preferred_element_type=jnp.float32,
    )


def _piece_kernel(rl_ref, rd_ref, x_ref, ol_ref, od_ref, *, nb, nh):
    @pl.when(pl.program_id(0) == 0)
    def _init():
        ol_ref[...] = jnp.zeros(ol_ref.shape, jnp.float32)
        od_ref[...] = jnp.zeros(od_ref.shape, jnp.float32)

    rows_l = rl_ref[...]
    rows_d = rd_ref[...]
    rn_l = jnp.sum(rows_l * rows_l, axis=1, keepdims=True)
    rn_d = jnp.sum(rows_d * rows_d, axis=1, keepdims=True)
    rows_l = -2.0 * rows_l
    rows_d = -2.0 * rows_d

    group = math.gcd(x_ref.shape[0], 8)

    def take(b, lo, width):
        return jnp.concatenate([x_ref[b * group + i, :, lo:lo + width] for i in range(group)], 1)

    def one_group(b, carry):
        acc_l, acc_d = carry
        cols = take(b, 0, nb)
        acc_l = acc_l + _accumulate(rows_l, rn_l, cols, take(b, nb, nb))
        cols = take(b, 2 * nb, nh)
        acc_d = acc_d + _accumulate(rows_d, rn_d, cols, take(b, 2 * nb + nh, nh))
        return acc_l, acc_d

    zero_l = jnp.zeros(ol_ref.shape, jnp.float32)
    zero_d = jnp.zeros(od_ref.shape, jnp.float32)
    acc_l, acc_d = lax.fori_loop(0, x_ref.shape[0] // group, one_group, (zero_l, zero_d))
    ol_ref[...] += acc_l
    od_ref[...] += acc_d


def apply_piece(rows_low, rows_diff, piece, nb, nh, interpret=False):
    n, feats, width = piece.shape
    probes = piece.shape[1]
    per = min(n, 8)
    rl, rd = rows_low.shape[1], rows_diff.shape[1]
    kern = functools.partial(_piece_kernel, nb=nb, nh=nh)
    full = lambda shape: pl.BlockSpec(shape, lambda j: (0,) * len(shape))
    return pl.pallas_call(
        kern,
        grid=(n // per,),
        in_specs=[
            full((rl, feats)),
            full((rd, feats)),
            pl.BlockSpec((per, feats, width), lambda j: (j, 0, 0)),
        ],
        out_specs=[full((probes, rl)), full((probes, rd))],
        out_shape=[
            jax.ShapeDtypeStruct((probes, rl), jnp.float32),
            jax.ShapeDtypeStruct((probes, rd), jnp.float32),
        ],
        compiler_params=pltpu.CompilerParams(dimension_semantics=("arbitrary",)),
        interpret=interpret,
    )(rows_low.T, rows_diff.T, piece)


def gather_bits(x, axis, size, bits):
    me = lax.axis_index(axis)
    buf = x[None]
    for bit in bits:
        mask = 1 << bit
        other = lax.ppermute(buf, axis, [(i, i ^ mask) for i in range(size)])
        upper = ((me >> bit) & 1) == 1
        low = jnp.where(upper, other, buf)
        high = jnp.where(upper, buf, other)
        buf = jnp.concatenate([low, high], 0)
    k = len(bits)
    buf = buf.reshape((2,) * k + x.shape)
    order = sorted(range(k), key=lambda i: -bits[k - 1 - i])
    buf = buf.transpose(tuple(order) + tuple(range(k, k + x.ndim)))
    return buf.reshape((size,) + x.shape)


def per_device(low_sites, low_probes, high_probes, nested, inv_len_low, inv_len_diff):
    feats_n, rows_dev = low_sites.shape
    probes_n = low_probes.shape[0]
    highs_dev = high_probes.shape[1]
    grp_size = 1 << len(GRP_BITS)
    blk_size = 1 << len(BLK_BITS)

    packet = jnp.concatenate(
        [low_sites.reshape(-1), low_probes.reshape(-1), high_probes.reshape(-1), nested.astype(jnp.float32)]
    )
    got = gather_bits(packet, "grp", grp_size, GRP_BITS)
    cuts = [feats_n * rows_dev, probes_n * rows_dev, probes_n * highs_dev, highs_dev]
    pieces = []
    start = 0
    for c in cuts:
        pieces.append(got[:, start:start + c])
        start += c

    def unblock(piece, rows):
        return piece.reshape(grp_size, rows, -1).transpose(1, 0, 2).reshape(rows, -1)

    feats_block = unblock(pieces[0], feats_n)
    lowp_block = unblock(pieces[1], probes_n)
    highp_block = unblock(pieces[2], probes_n)
    nest_block = pieces[3].reshape(-1).astype(jnp.int32)

    width = feats_block.shape[1]
    base = lax.axis_index("blk") * width
    place_block = nest_block - base
    slots = lax.broadcasted_iota(jnp.int32, (width,), 0)
    pick = (slots[:, None] == place_block[None, :]).astype(jnp.float32)
    high_feats_block = jnp.dot(
        feats_block, pick, precision=lax.Precision.HIGHEST, preferred_element_type=jnp.float32
    )
    spread = lax.dot_general(
        highp_block, pick, (((1,), (1,)), ((), ())),
        precision=lax.Precision.HIGHEST, preferred_element_type=jnp.float32,
    )
    mixed_block = lowp_block + RHO * spread

    own_high = lax.axis_index("grp") * highs_dev
    high_feats = lax.dynamic_slice_in_dim(high_feats_block, own_high, highs_dev, 1)

    wide = jnp.concatenate(
        [feats_block * inv_len_low[:, None], mixed_block, high_feats_block * inv_len_diff[:, None], highp_block], 1
    )
    nb = width
    nh = high_feats_block.shape[1]
    rows_low = jnp.concatenate([low_sites, high_feats], 1) * inv_len_low[:, None]
    rows_diff = high_feats * inv_len_diff[:, None]

    buf = wide[None]
    new_low, new_diff = apply_piece(rows_low, rows_diff, buf, nb, nh)
    for bit in BLK_BITS:
        mask = 1 << bit
        other = lax.ppermute(buf, "blk", [(i, i ^ mask) for i in range(blk_size)])
        part_low, part_diff = apply_piece(rows_low, rows_diff, other, nb, nh)
        new_low = new_low + part_low
        new_diff = new_diff + part_diff
        if bit != BLK_BITS[-1]:
            buf = jnp.concatenate([buf, other], 0)
    new_diff = VAR_DIFF * new_diff
    high_part = new_low[:, rows_dev:]
    high_out = RHO * high_part + new_diff
    return (new_low[:, :rows_dev], high_out)


def solution(mesh):
    return jax.shard_map(
        per_device,
        mesh=mesh,
        in_specs=(
            P(None, ("blk", "grp")),
            P(None, ("blk", "grp")),
            P(None, ("blk", "grp")),
            P(("blk", "grp")),
            P(),
            P(),
        ),
        out_specs=(P(None, ("blk", "grp")), P(None, ("blk", "grp"))),
        check_vma=False,
    )
```
